512 devices in a mesh: dp: 32 (over z, y_lo, core), feat: 16 (over y_hi, x).
Axes of the slice: x: 4, y: 8 (y_hi: 4, y_lo: 2; y = y_hi * 2 + y_lo), z: 8, core: 2. Of those that a mesh axis runs over, the one named last changes fastest.
Arguments:
- tokens: bfloat16 [8192, 8192], P('dp', 'feat'), may hold values from -6 to 6
- up_left: bfloat16 [16, 512, 2048], P('feat', 'dp'), may hold values from -0.25 to 0.25
- up_right: bfloat16 [2048, 16, 16], P('feat'), may hold values from -1.5 to 1.5
- down_left: bfloat16 [16, 2048, 512], P('feat', 'dp'), may hold values from -0.125 to 0.125
- down_right: bfloat16 [512, 16, 16], P('feat'), may hold values from -1.5 to 1.5
- layer_grad: bfloat16 [8192, 8192], P('dp', 'feat'), may hold values from -6 to 6
Outputs:
- layer_out: bfloat16 [8192, 8192], P('dp', 'feat')
- grad_tokens: bfloat16 [8192, 8192], P('dp', 'feat')
- grad_up_left: float32 [16, 512, 2048], P('feat', 'dp')
- grad_up_right: float32 [2048, 16, 16], P('feat')
- grad_down_left: float32 [16, 2048, 512], P('feat', 'dp')
- grad_down_right: float32 [512, 16, 16], P('feat')
The draws below stay inside these ranges and needn't reach their ends.
All inputs are finite; a program needn't handle non-finite values.
Results may differ from the reference program's by a relative error of at most 0.0067.
Values may be sent and summed in bfloat16 or wider, within the bound.
No kernel may reach another device: no remote copies, remote signals or barrier semaphores. Data moves between devices by JAX's collectives and lax.ppermute only.
A program may use at most 128 MiB of HBM per device.

```python
import jax
import jax.numpy as jnp
from jax import lax

D = 8192
H = 32768
BLOCK = 512
BLOCKS = 16
HID_BLOCK = 2048
TILE_UP = 128
TILE_DOWN = 32
TOK_DEV = 256
TOKENS = 8192
N_DP = 32


def block_scale(rng, extent, shards, low, high):
    level, own = 1.0, jax.random.fold_in(rng, 6)
    for dim, shards_of in shards:
        heights = jnp.exp(jax.random.uniform(jax.random.fold_in(own, dim), (shards_of,), jnp.float32, low / len(shards), high / len(shards)))
        level = level * jnp.repeat(heights, extent[dim] // shards_of).reshape([-1 if axis == dim else 1 for axis in range(len(extent))])
    return level


def centred(own_key, dims, scale, bound, split=(), kind=jnp.bfloat16):
    gain = block_scale(own_key, dims, split, -0.22, 0.18) if split else 1.0
    array = jax.random.normal(own_key, dims, jnp.float32) * scale * gain
    return jnp.minimum(jnp.maximum(array, -bound), bound).astype(kind)


def setup_inputs(seed: int = 0) -> dict:
    keys = jax.random.split(jax.random.key(seed), 7)
    tokens = centred(keys[0], (TOKENS, D), 1.0, 6.0, ((0, 32), (1, 16)))
    up_left = centred(keys[1], (BLOCKS, BLOCK, HID_BLOCK), BLOCK ** -0.5, 0.25, ((0, 16), (1, 32)))
    up_right = centred(keys[2], (HID_BLOCK, BLOCKS, BLOCKS), BLOCKS ** -0.5, 1.5, ((0, 16),))
    down_left = centred(keys[3], (BLOCKS, HID_BLOCK, BLOCK), HID_BLOCK ** -0.5, 0.125, ((0, 16), (1, 32)))
    down_right = centred(keys[4], (BLOCK, BLOCKS, BLOCKS), BLOCKS ** -0.5, 1.5, ((0, 16),))
    layer_grad = centred(keys[5], (TOKENS, D), 1.0, 6.0, ((0, 32), (1, 16)))
    return {"tokens": tokens, "up_left": up_left, "up_right": up_right, "down_left": down_left, "down_right": down_right, "layer_grad": layer_grad}


def to_hidden(values):
    count = values.shape[0]
    shaped = values.reshape(count, HID_BLOCK // TILE_UP, TILE_UP, BLOCKS).transpose(0, 1, 3, 2)
    return shaped.reshape(count, H)


def from_hidden(values):
    count = values.shape[0]
    shaped = values.reshape(count, HID_BLOCK // TILE_UP, BLOCKS, TILE_UP).transpose(0, 1, 3, 2)
    return shaped.reshape(count, HID_BLOCK, BLOCKS)


def to_features(values):
    count = values.shape[0]
    shaped = values.reshape(count, BLOCK // TILE_DOWN, TILE_DOWN, BLOCKS).transpose(0, 1, 3, 2)
    return shaped.reshape(count, D)


def from_features(values):
    count = values.shape[0]
    shaped = values.reshape(count, BLOCK // TILE_DOWN, BLOCKS, TILE_DOWN).transpose(0, 1, 3, 2)
    return shaped.reshape(count, BLOCK, BLOCKS)


def reference(tokens, up_left, up_right, down_left, down_right, layer_grad):
    wide = jnp.float32
    up_left_wide = up_left.astype(wide)
    up_right_wide = up_right.astype(wide)
    down_left_wide = down_left.astype(wide)
    down_right_wide = down_right.astype(wide)
    grad_scale = float(TOKENS) ** -0.5

    def one_group(carry, inputs):
        sum_up_left, sum_up_right, sum_down_left, sum_down_right = carry
        token_rows, grad_rows = inputs
        count = token_rows.shape[0]
        token_blocks = token_rows.reshape(count, BLOCKS, BLOCK).astype(wide)
        up_inner = jnp.einsum('tji,jig->tjg', token_blocks, up_left_wide).astype(jnp.bfloat16)
        preact = jnp.einsum('tjg,gjk->tgk', up_inner.astype(wide), up_right_wide)
        sigmoid_val = jax.nn.sigmoid(preact)
        hidden = to_hidden(preact * sigmoid_val).astype(jnp.bfloat16)
        hidden_blocks = hidden.reshape(count, BLOCKS, HID_BLOCK).astype(wide)
        down_inner = jnp.einsum('tbh,bhc->tbc', hidden_blocks, down_left_wide).astype(jnp.bfloat16)
        mixed = jnp.einsum('tjc,cjk->tck', down_inner.astype(wide), down_right_wide)
        layer_out = to_features(mixed).astype(jnp.bfloat16)
        grad_mixed = from_features(grad_rows).astype(wide)
        grad_down_inner = jnp.einsum('tck,cjk->tjc', grad_mixed, down_right_wide).astype(jnp.bfloat16)
        term_down_right = jnp.einsum('tjc,tck->cjk', down_inner.astype(wide), grad_mixed) * grad_scale
        term_down_left = jnp.einsum('tbh,tbc->bhc', hidden_blocks, grad_down_inner.astype(wide)) * grad_scale
        grad_hidden = jnp.einsum('tbc,bhc->tbh', grad_down_inner.astype(wide), down_left_wide).reshape(count, H)
        grad_hidden_groups = from_hidden(grad_hidden)
        grad_preact = (grad_hidden_groups * sigmoid_val * (1.0 + preact * (1.0 - sigmoid_val))).astype(jnp.bfloat16)
        grad_up_inner = jnp.einsum('tgk,gjk->tjg', grad_preact.astype(wide), up_right_wide).astype(jnp.bfloat16)
        term_up_right = jnp.einsum('tjg,tgk->gjk', up_inner.astype(wide), grad_preact.astype(wide)) * grad_scale
        grad_tokens = jnp.einsum('tjg,jig->tji', grad_up_inner.astype(wide), up_left_wide).astype(jnp.bfloat16)
        term_up_left = jnp.einsum('tji,tjg->jig', token_blocks, grad_up_inner.astype(wide)) * grad_scale
        new_carry = (sum_up_left + term_up_left, sum_up_right + term_up_right,
                     sum_down_left + term_down_left, sum_down_right + term_down_right)
        return new_carry, (layer_out, grad_tokens.reshape(count, D))

    start = (jnp.zeros((BLOCKS, BLOCK, HID_BLOCK), wide), jnp.zeros((HID_BLOCK, BLOCKS, BLOCKS), wide),
             jnp.zeros((BLOCKS, HID_BLOCK, BLOCK), wide), jnp.zeros((BLOCK, BLOCKS, BLOCKS), wide))
    token_groups = tokens.reshape(N_DP, TOK_DEV, D)
    grad_groups = layer_grad.reshape(N_DP, TOK_DEV, D)
    final, (outputs, token_grads) = lax.scan(one_group, start, (token_groups, grad_groups))
    grad_up_left, grad_up_right, grad_down_left, grad_down_right = final
    return (outputs.reshape(TOKENS, D), token_grads.reshape(TOKENS, D),
            grad_up_left, grad_up_right, grad_down_left, grad_down_right)
```

```python
import jax
import jax.numpy as jnp
import numpy as np
from jax import lax
from jax.sharding import Mesh
from jax.sharding import PartitionSpec as P

TILE_UP = 128
TILE_DOWN = 32

DP_AXES = ("z", "ylo", "core")
FEAT_AXES = ("yhi", "x")


def split_mesh(mesh):
    n_dp = mesh.shape["dp"]
    n_feat = mesh.shape["feat"]
    sizes = (n_dp // 4, 2, 2, n_feat // 4, 4)
    devices = np.asarray(mesh.devices).reshape(sizes)
    return Mesh(devices, DP_AXES + FEAT_AXES)


def exchange(wired):
    rows, feat_count, piece = wired.shape
    n_x = lax.axis_size("x")
    n_y = feat_count // n_x
    shaped = wired.reshape(rows, n_y, n_x, piece)
    shaped = lax.all_to_all(shaped, "x", 2, 2, tiled=True)
    shaped = lax.all_to_all(shaped, "yhi", 1, 1, tiled=True)
    return shaped.reshape(rows, feat_count, piece)


def dp_reduce_scatter(part, row_axis):
    shape = part.shape
    rows = shape[row_axis]
    n_z = lax.axis_size("z")
    split = shape[:row_axis] + (n_z, 2, 2, rows // (4 * n_z)) + shape[row_axis + 1 :]
    x = part.reshape(split)
    x = lax.psum_scatter(x, "core", scatter_dimension=row_axis + 2, tiled=True)
    x = lax.psum_scatter(x, "z", scatter_dimension=row_axis, tiled=True)
    x = lax.psum_scatter(x, "ylo", scatter_dimension=row_axis + 1, tiled=True)
    return x.reshape(shape[:row_axis] + (rows // (4 * n_z),) + shape[row_axis + 1 :])


def dp_all_gather(local, row_axis):
    shape = local.shape
    rows = shape[row_axis]
    x = local.reshape(shape[:row_axis] + (1, 1, 1, rows) + shape[row_axis + 1 :])
    x = lax.all_gather(x, "ylo", axis=row_axis + 1, tiled=True)
    x = lax.all_gather(x, "z", axis=row_axis, tiled=True)
    x = lax.all_gather(x, "core", axis=row_axis + 2, tiled=True)
    total = x.shape[row_axis] * x.shape[row_axis + 1] * x.shape[row_axis + 2] * rows
    return x.reshape(shape[:row_axis] + (total,) + shape[row_axis + 1 :])


def to_wire(blocks, feat_count):
    tok_rows, local_blocks, full_width = blocks.shape
    piece = full_width // feat_count
    shaped = blocks.reshape(tok_rows, local_blocks, feat_count, piece).transpose(0, 2, 1, 3)
    return shaped.reshape(tok_rows, feat_count, local_blocks * piece)


def from_wire(wired, local_blocks):
    tok_rows, feat_count, line_len = wired.shape
    piece = line_len // local_blocks
    shaped = wired.reshape(tok_rows, feat_count, local_blocks, piece).transpose(0, 2, 1, 3)
    return shaped.reshape(tok_rows, local_blocks, feat_count * piece)


def on_device(tokens, up_left, up_right, down_left, down_right, layer_grad):
    tok_rows = tokens.shape[0]
    local_blocks = up_left.shape[0]
    hidden_width = up_left.shape[2]
    block_width = down_left.shape[2]
    blocks_all = up_right.shape[1]
    group_up = up_right.shape[0]
    group_down = down_right.shape[0]
    feat_count = lax.axis_size("yhi") * lax.axis_size("x")
    n_dp = lax.axis_size("z") * lax.axis_size("ylo") * lax.axis_size("core")
    grad_scale = float(tok_rows * n_dp) ** (-0.5)
    tiles_up = group_up // TILE_UP
    tiles_down = group_down // TILE_DOWN
    up_full = dp_all_gather(up_left, 1)
    token_blocks = tokens.reshape(tok_rows, local_blocks, block_width)
    up_inner = jnp.einsum(
        "tbi,big->tbg", token_blocks, up_full, preferred_element_type=jnp.float32
    ).astype(jnp.bfloat16)
    up_mixed = exchange(to_wire(up_inner, feat_count))
    preact = jnp.einsum("tjg,gjk->tkg", up_mixed, up_right, preferred_element_type=jnp.float32)
    sigmoid_val = jax.nn.sigmoid(preact)
    activated = (
        (preact * sigmoid_val)
        .reshape(tok_rows, blocks_all, tiles_up, TILE_UP)
        .transpose(0, 2, 1, 3)
    )
    hidden = activated.reshape(tok_rows, local_blocks, hidden_width).astype(jnp.bfloat16)
    down_full = dp_all_gather(down_left, 1)
    down_inner = jnp.einsum(
        "tbh,bhc->tbc", hidden, down_full, preferred_element_type=jnp.float32
    ).astype(jnp.bfloat16)
    down_mixed = exchange(to_wire(down_inner, feat_count)).reshape(
        tok_rows, blocks_all * group_down
    )
    identity = jnp.eye(group_down, dtype=jnp.bfloat16).reshape(group_down, tiles_down, TILE_DOWN)
    mix_matrix = jnp.einsum(
        "cjk,cal->jcakl", down_right, identity, preferred_element_type=jnp.float32
    )
    mix_matrix = mix_matrix.astype(jnp.bfloat16).reshape(
        blocks_all * group_down, blocks_all * group_down
    )
    layer_out = jnp.dot(down_mixed, mix_matrix, preferred_element_type=jnp.float32).astype(
        jnp.bfloat16
    )
    grad_down_mixed = lax.dot_general(
        layer_grad, mix_matrix, (((1,), (1,)), ((), ())), preferred_element_type=jnp.float32
    ).astype(jnp.bfloat16)
    grad_by_group = layer_grad.reshape(tok_rows, tiles_down, blocks_all, TILE_DOWN).transpose(
        0, 2, 1, 3
    )
    grad_by_group = grad_by_group.reshape(tok_rows, blocks_all, group_down)
    right_down_term = (
        jnp.einsum(
            "tjc,tkc->cjk",
            down_mixed.reshape(tok_rows, blocks_all, group_down),
            grad_by_group,
            preferred_element_type=jnp.float32,
        )
        * grad_scale
    )
    grad_down_inner = from_wire(
        exchange(grad_down_mixed.reshape(tok_rows, feat_count, local_blocks * group_down)),
        local_blocks,
    )
    grad_down_left = dp_reduce_scatter(
        jnp.einsum("tbh,tbc->hbc", hidden, grad_down_inner, preferred_element_type=jnp.float32)
        * grad_scale,
        0,
    ).transpose(1, 0, 2)
    grad_hidden = jnp.einsum(
        "tbc,bhc->tbh", grad_down_inner, down_full, preferred_element_type=jnp.float32
    )
    grad_hidden = grad_hidden.reshape(tok_rows, tiles_up, blocks_all, TILE_UP).transpose(0, 2, 1, 3)
    grad_hidden = grad_hidden.reshape(tok_rows, blocks_all, group_up)
    grad_preact = (grad_hidden * sigmoid_val * (1.0 + preact * (1.0 - sigmoid_val))).astype(
        jnp.bfloat16
    )
    grad_up_mixed = jnp.einsum(
        "tkg,gjk->tjg", grad_preact, up_right, preferred_element_type=jnp.float32
    ).astype(jnp.bfloat16)
    right_up_term = (
        jnp.einsum("tjg,tkg->gjk", up_mixed, grad_preact, preferred_element_type=jnp.float32)
        * grad_scale
    )
    grad_up_inner = from_wire(exchange(grad_up_mixed), local_blocks)
    grad_tokens = jnp.einsum(
        "tbg,big->tbi", grad_up_inner, up_full, preferred_element_type=jnp.float32
    ).astype(jnp.bfloat16)
    grad_tokens = grad_tokens.reshape(tok_rows, local_blocks * block_width)
    grad_up_left = dp_reduce_scatter(
        jnp.einsum("tbi,tbg->ibg", token_blocks, grad_up_inner, preferred_element_type=jnp.float32)
        * grad_scale,
        0,
    ).transpose(1, 0, 2)
    rights = jnp.concatenate([right_up_term, right_down_term], axis=0)
    rights = lax.psum(rights, DP_AXES)
    grad_up_right = rights[:group_up]
    grad_down_right = rights[group_up:]
    return (layer_out, grad_tokens, grad_up_left, grad_up_right, grad_down_left, grad_down_right)


def solution(mesh):
    fine = split_mesh(mesh)
    row = P(DP_AXES, FEAT_AXES)
    weight = P(FEAT_AXES, DP_AXES, None)
    mixer = P(FEAT_AXES, None, None)
    return jax.shard_map(
        on_device,
        mesh=fine,
        in_specs=(row, weight, mixer, weight, mixer, row),
        out_specs=(row, row, weight, mixer, weight, mixer),
        check_vma=False,
    )
```

```python
import jax
import jax.numpy as jnp
import numpy as np
from jax import lax
from jax.sharding import Mesh
from jax.sharding import PartitionSpec as P

TILE_UP = 128
TILE_DOWN = 32

DP_AXES = ("z", "ylo", "core")
FEAT_AXES = ("yhi", "x")


def split_mesh(mesh):
    n_dp = mesh.shape["dp"]
    n_feat = mesh.shape["feat"]
    sizes = (n_dp // 4, 2, 2, n_feat // 4, 4)
    devices = np.asarray(mesh.devices).reshape(sizes)
    return Mesh(devices, DP_AXES + FEAT_AXES)


def exchange(wired):
    rows, feat_count, piece = wired.shape
    n_x = lax.axis_size("x")
    n_y = feat_count // n_x
    shaped = wired.reshape(rows, n_y, n_x, piece)
    shaped = lax.all_to_all(shaped, "x", 2, 2, tiled=True)
    shaped = lax.all_to_all(shaped, "yhi", 1, 1, tiled=True)
    return shaped.reshape(rows, feat_count, piece)


def shift(value, axis, step):
    n = lax.axis_size(axis)
    return lax.ppermute(value, axis, [(i, (i + step) % n) for i in range(n)])


def swap(value, axis, mask):
    n = lax.axis_size(axis)
    return lax.ppermute(value, axis, [(i, i ^ mask) for i in range(n)])


def z_ring_reduce_scatter(x):
    n = x.shape[0]
    me = lax.axis_index("z")
    lo, hi = jnp.split(x, 2, axis=-1)
    fwd = None
    bwd = None
    for step in range(1, n):
        own_f = lax.dynamic_index_in_dim(lo, (me - step) % n, 0, keepdims=False)
        own_b = lax.dynamic_index_in_dim(hi, (me + step) % n, 0, keepdims=False)
        fwd = shift(own_f if fwd is None else fwd + own_f, "z", 1)
        bwd = shift(own_b if bwd is None else bwd + own_b, "z", -1)
    fwd = fwd + lax.dynamic_index_in_dim(lo, me, 0, keepdims=False)
    bwd = bwd + lax.dynamic_index_in_dim(hi, me, 0, keepdims=False)
    return jnp.concatenate([fwd, bwd], axis=-1)


def z_ring_all_gather(chunk):
    n = lax.axis_size("z")
    me = lax.axis_index("z")
    out = jnp.zeros((n,) + chunk.shape, chunk.dtype)
    out = lax.dynamic_update_index_in_dim(out, chunk, me, 0)
    fwd = chunk
    bwd = chunk
    half = n // 2
    for step in range(1, half):
        fwd = shift(fwd, "z", 1)
        bwd = shift(bwd, "z", -1)
        out = lax.dynamic_update_index_in_dim(out, fwd, (me - step) % n, 0)
        out = lax.dynamic_update_index_in_dim(out, bwd, (me + step) % n, 0)
    lo, _ = jnp.split(fwd, 2, axis=-1)
    _, hi = jnp.split(bwd, 2, axis=-1)
    last = jnp.concatenate([shift(lo, "z", 1), shift(hi, "z", -1)], axis=-1)
    out = lax.dynamic_update_index_in_dim(out, last, (me + half) % n, 0)
    return out


def dp_reduce_scatter(part):
    rows = part.shape[0]
    rest = part.shape[1:]
    n_z = lax.axis_size("z")
    x = part.reshape((n_z, 2, 2, rows // (4 * n_z)) + rest)
    core = lax.axis_index("core")
    mine = lax.dynamic_index_in_dim(x, core, 2, keepdims=False)
    other = lax.dynamic_index_in_dim(x, 1 - core, 2, keepdims=False)
    x = mine + swap(other, "core", 1)
    x = z_ring_reduce_scatter(x)
    ylo = lax.axis_index("ylo")
    mine = lax.dynamic_index_in_dim(x, ylo, 0, keepdims=False)
    other = lax.dynamic_index_in_dim(x, 1 - ylo, 0, keepdims=False)
    return mine + swap(other, "ylo", 1)


def dp_all_gather(local):
    ylo = lax.axis_index("ylo")
    got = swap(local, "ylo", 1)
    pair = jnp.where(ylo == 0, jnp.stack([local, got]), jnp.stack([got, local]))
    ring = z_ring_all_gather(pair)
    core = lax.axis_index("core")
    other = swap(ring, "core", 1)
    both = jnp.where(core == 0, jnp.stack([ring, other], 2), jnp.stack([other, ring], 2))
    return both.reshape((-1,) + local.shape[1:])


def dp_all_reduce(x):
    x = x + swap(x, "core", 1)
    x = x + swap(x, "ylo", 1)
    mask = 1
    while mask < lax.axis_size("z"):
        x = x + swap(x, "z", mask)
        mask *= 2
    return x


def to_wire(blocks, feat_count):
    tok_rows, local_blocks, full_width = blocks.shape
    piece = full_width // feat_count
    shaped = blocks.reshape(tok_rows, local_blocks, feat_count, piece).transpose(0, 2, 1, 3)
    return shaped.reshape(tok_rows, feat_count, local_blocks * piece)


def from_wire(wired, local_blocks):
    tok_rows, feat_count, line_len = wired.shape
    piece = line_len // local_blocks
    shaped = wired.reshape(tok_rows, feat_count, local_blocks, piece).transpose(0, 2, 1, 3)
    return shaped.reshape(tok_rows, local_blocks, feat_count * piece)


def on_device(tokens, up_left, up_right, down_left, down_right, layer_grad):
    tok_rows = tokens.shape[0]
    local_blocks = up_left.shape[0]
    hidden_width = up_left.shape[2]
    block_width = down_left.shape[2]
    blocks_all = up_right.shape[1]
    group_up = up_right.shape[0]
    group_down = down_right.shape[0]
    feat_count = lax.axis_size("yhi") * lax.axis_size("x")
    n_dp = lax.axis_size("z") * lax.axis_size("ylo") * lax.axis_size("core")
    grad_scale = float(tok_rows * n_dp) ** (-0.5)
    tiles_up = group_up // TILE_UP
    tiles_down = group_down // TILE_DOWN
    up_full = dp_all_gather(up_left[0])[None]
    token_blocks = tokens.reshape(tok_rows, local_blocks, block_width)
    up_inner = jnp.einsum(
        "tbi,big->tbg", token_blocks, up_full, preferred_element_type=jnp.float32
    ).astype(jnp.bfloat16)
    up_mixed = exchange(to_wire(up_inner, feat_count))
    preact = jnp.einsum("tjg,gjk->tkg", up_mixed, up_right, preferred_element_type=jnp.float32)
    sigmoid_val = jax.nn.sigmoid(preact)
    activated = (
        (preact * sigmoid_val)
        .reshape(tok_rows, blocks_all, tiles_up, TILE_UP)
        .transpose(0, 2, 1, 3)
    )
    hidden = activated.reshape(tok_rows, local_blocks, hidden_width).astype(jnp.bfloat16)
    down_full = dp_all_gather(down_left[0])[None]
    down_inner = jnp.einsum(
        "tbh,bhc->tbc", hidden, down_full, preferred_element_type=jnp.float32
    ).astype(jnp.bfloat16)
    down_mixed = exchange(to_wire(down_inner, feat_count)).reshape(
        tok_rows, blocks_all * group_down
    )
    identity = jnp.eye(group_down, dtype=jnp.bfloat16).reshape(group_down, tiles_down, TILE_DOWN)
    mix_matrix = jnp.einsum(
        "cjk,cal->jcakl", down_right, identity, preferred_element_type=jnp.float32
    )
    mix_matrix = mix_matrix.astype(jnp.bfloat16).reshape(
        blocks_all * group_down, blocks_all * group_down
    )
    layer_out = jnp.dot(down_mixed, mix_matrix, preferred_element_type=jnp.float32).astype(
        jnp.bfloat16
    )
    grad_down_mixed = lax.dot_general(
        layer_grad, mix_matrix, (((1,), (1,)), ((), ())), preferred_element_type=jnp.float32
    ).astype(jnp.bfloat16)
    grad_by_group = layer_grad.reshape(tok_rows, tiles_down, blocks_all, TILE_DOWN).transpose(
        0, 2, 1, 3
    )
    grad_by_group = grad_by_group.reshape(tok_rows, blocks_all, group_down)
    right_down_term = (
        jnp.einsum(
            "tjc,tkc->cjk",
            down_mixed.reshape(tok_rows, blocks_all, group_down),
            grad_by_group,
            preferred_element_type=jnp.float32,
        )
        * grad_scale
    )
    grad_down_inner = from_wire(
        exchange(grad_down_mixed.reshape(tok_rows, feat_count, local_blocks * group_down)),
        local_blocks,
    )
    grad_down_left = dp_reduce_scatter(
        jnp.einsum("tbh,tbc->hbc", hidden, grad_down_inner, preferred_element_type=jnp.float32)
        * grad_scale
    ).transpose(1, 0, 2)
    grad_hidden = jnp.einsum(
        "tbc,bhc->tbh", grad_down_inner, down_full, preferred_element_type=jnp.float32
    )
    grad_hidden = grad_hidden.reshape(tok_rows, tiles_up, blocks_all, TILE_UP).transpose(0, 2, 1, 3)
    grad_hidden = grad_hidden.reshape(tok_rows, blocks_all, group_up)
    grad_preact = (grad_hidden * sigmoid_val * (1.0 + preact * (1.0 - sigmoid_val))).astype(
        jnp.bfloat16
    )
    grad_up_mixed = jnp.einsum(
        "tkg,gjk->tjg", grad_preact, up_right, preferred_element_type=jnp.float32
    ).astype(jnp.bfloat16)
    right_up_term = (
        jnp.einsum("tjg,tkg->gjk", up_mixed, grad_preact, preferred_element_type=jnp.float32)
        * grad_scale
    )
    grad_up_inner = from_wire(exchange(grad_up_mixed), local_blocks)
    grad_tokens = jnp.einsum(
        "tbg,big->tbi", grad_up_inner, up_full, preferred_element_type=jnp.float32
    ).astype(jnp.bfloat16)
    grad_tokens = grad_tokens.reshape(tok_rows, local_blocks * block_width)
    grad_up_left = dp_reduce_scatter(
        jnp.einsum("tbi,tbg->ibg", token_blocks, grad_up_inner, preferred_element_type=jnp.float32)
        * grad_scale
    ).transpose(1, 0, 2)
    rights = jnp.concatenate([right_up_term, right_down_term], axis=0)
    rights = dp_all_reduce(rights)
    grad_up_right = rights[:group_up]
    grad_down_right = rights[group_up:]
    return (layer_out, grad_tokens, grad_up_left, grad_up_right, grad_down_left, grad_down_right)


def solution(mesh):
    fine = split_mesh(mesh)
    row = P(DP_AXES, FEAT_AXES)
    weight = P(FEAT_AXES, DP_AXES, None)
    mixer = P(FEAT_AXES, None, None)
    return jax.shard_map(
        on_device,
        mesh=fine,
        in_specs=(row, weight, mixer, weight, mixer, row),
        out_specs=(row, row, weight, mixer, weight, mixer),
        check_vma=False,
    )
```

```python
import jax
import jax.numpy as jnp
import numpy as np
from jax import lax
from jax.sharding import Mesh
from jax.sharding import PartitionSpec as P

TILE_UP = 128
TILE_DOWN = 32

DP_AXES = ("z", "ylo", "core")
FEAT_AXES = ("yhi", "x")


def split_mesh(mesh):
    n_dp = mesh.shape["dp"]
    n_feat = mesh.shape["feat"]
    sizes = (n_dp // 4, 2, 2, n_feat // 4, 4)
    devices = np.asarray(mesh.devices).reshape(sizes)
    return Mesh(devices, DP_AXES + FEAT_AXES)


def exchange(wired):
    rows, feat_count, piece = wired.shape
    n_x = lax.axis_size("x")
    n_y = feat_count // n_x
    shaped = wired.reshape(rows, n_y, n_x, piece)
    shaped = lax.all_to_all(shaped, "x", 2, 2, tiled=True)
    shaped = lax.all_to_all(shaped, "yhi", 1, 1, tiled=True)
    return shaped.reshape(rows, feat_count, piece)


def shift(value, axis, step):
    n = lax.axis_size(axis)
    return lax.ppermute(value, axis, [(i, (i + step) % n) for i in range(n)])


def swap(value, axis, mask):
    n = lax.axis_size(axis)
    return lax.ppermute(value, axis, [(i, i ^ mask) for i in range(n)])


def z_ring_reduce_scatter(x):
    n = x.shape[0]
    me = lax.axis_index("z")
    lo, hi = jnp.split(x, 2, axis=-1)
    fwd = None
    bwd = None
    for step in range(1, n):
        own_f = lax.dynamic_index_in_dim(lo, (me - step) % n, 0, keepdims=False)
        own_b = lax.dynamic_index_in_dim(hi, (me + step) % n, 0, keepdims=False)
        fwd = shift(own_f if fwd is None else fwd + own_f, "z", 1)
        bwd = shift(own_b if bwd is None else bwd + own_b, "z", -1)
    fwd = fwd + lax.dynamic_index_in_dim(lo, me, 0, keepdims=False)
    bwd = bwd + lax.dynamic_index_in_dim(hi, me, 0, keepdims=False)
    return jnp.concatenate([fwd, bwd], axis=-1)


def z_ring_all_gather(chunk):
    n = lax.axis_size("z")
    me = lax.axis_index("z")
    out = jnp.zeros((n,) + chunk.shape, chunk.dtype)
    out = lax.dynamic_update_index_in_dim(out, chunk, me, 0)
    fwd = chunk
    bwd = chunk
    half = n // 2
    for step in range(1, half):
        fwd = shift(fwd, "z", 1)
        bwd = shift(bwd, "z", -1)
        out = lax.dynamic_update_index_in_dim(out, fwd, (me - step) % n, 0)
        out = lax.dynamic_update_index_in_dim(out, bwd, (me + step) % n, 0)
    lo, _ = jnp.split(fwd, 2, axis=-1)
    _, hi = jnp.split(bwd, 2, axis=-1)
    last = jnp.concatenate([shift(lo, "z", 1), shift(hi, "z", -1)], axis=-1)
    out = lax.dynamic_update_index_in_dim(out, last, (me + half) % n, 0)
    return out


def dp_reduce_scatter(part):
    rows = part.shape[0]
    rest = part.shape[1:]
    n_z = lax.axis_size("z")
    x = part.reshape((n_z, 2, 2, rows // (4 * n_z)) + rest)
    core = lax.axis_index("core")
    mine = lax.dynamic_index_in_dim(x, core, 2, keepdims=False)
    other = lax.dynamic_index_in_dim(x, 1 - core, 2, keepdims=False)
    x = mine + swap(other, "core", 1)
    x = z_ring_reduce_scatter(x)
    ylo = lax.axis_index("ylo")
    mine = lax.dynamic_index_in_dim(x, ylo, 0, keepdims=False)
    other = lax.dynamic_index_in_dim(x, 1 - ylo, 0, keepdims=False)
    return mine + swap(other, "ylo", 1)


def dp_all_gather(local):
    ylo = lax.axis_index("ylo")
    got = swap(local, "ylo", 1)
    pair = jnp.where(ylo == 0, jnp.stack([local, got]), jnp.stack([got, local]))
    ring = z_ring_all_gather(pair)
    core = lax.axis_index("core")
    other = swap(ring, "core", 1)
    both = jnp.where(core == 0, jnp.stack([ring, other], 2), jnp.stack([other, ring], 2))
    return both.reshape((-1,) + local.shape[1:])


def dp_all_reduce(x):
    x = x + swap(x, "core", 1)
    x = x + swap(x, "ylo", 1)
    mask = 1
    while mask < lax.axis_size("z"):
        x = x + swap(x, "z", mask)
        mask *= 2
    return x


def to_wire(blocks, feat_count):
    tok_rows, local_blocks, full_width = blocks.shape
    piece = full_width // feat_count
    shaped = blocks.reshape(tok_rows, local_blocks, feat_count, piece).transpose(0, 2, 1, 3)
    return shaped.reshape(tok_rows, feat_count, local_blocks * piece)


def from_wire(wired, local_blocks):
    tok_rows, feat_count, line_len = wired.shape
    piece = line_len // local_blocks
    shaped = wired.reshape(tok_rows, feat_count, local_blocks, piece).transpose(0, 2, 1, 3)
    return shaped.reshape(tok_rows, local_blocks, feat_count * piece)


def on_device(tokens, up_left, up_right, down_left, down_right, layer_grad):
    tok_rows = tokens.shape[0]
    local_blocks = up_left.shape[0]
    hidden_width = up_left.shape[2]
    block_width = down_left.shape[2]
    blocks_all = up_right.shape[1]
    group_up = up_right.shape[0]
    group_down = down_right.shape[0]
    feat_count = lax.axis_size("yhi") * lax.axis_size("x")
    n_dp = lax.axis_size("z") * lax.axis_size("ylo") * lax.axis_size("core")
    grad_scale = float(tok_rows * n_dp) ** (-0.5)
    tiles_up = group_up // TILE_UP
    tiles_down = group_down // TILE_DOWN
    hidden_rows = down_left.shape[1]
    up_rows = up_left.shape[1]
    weights = jnp.concatenate(
        [up_left[0], down_left[0].reshape(up_rows, hidden_rows * block_width // up_rows)], axis=1
    )
    weights = dp_all_gather(weights)
    up_full = weights[:, :hidden_width][None]
    down_full = weights[:, hidden_width:].reshape(1, -1, block_width)
    token_blocks = tokens.reshape(tok_rows, local_blocks, block_width)
    identity = jnp.eye(group_down, dtype=jnp.bfloat16).reshape(group_down, tiles_down, TILE_DOWN)
    mix_matrix = jnp.einsum(
        "cjk,cal->jcakl", down_right, identity, preferred_element_type=jnp.float32
    )
    mix_matrix = mix_matrix.astype(jnp.bfloat16).reshape(
        blocks_all * group_down, blocks_all * group_down
    )
    grad_down_mixed = lax.dot_general(
        layer_grad, mix_matrix, (((1,), (1,)), ((), ())), preferred_element_type=jnp.float32
    ).astype(jnp.bfloat16)
    up_inner = jnp.einsum(
        "tbi,big->tbg", token_blocks, up_full, preferred_element_type=jnp.float32
    ).astype(jnp.bfloat16)
    up_piece = hidden_width // feat_count
    first = exchange(
        jnp.concatenate(
            [
                to_wire(up_inner, feat_count),
                grad_down_mixed.reshape(tok_rows, feat_count, local_blocks * group_down),
            ],
            axis=2,
        )
    )
    up_mixed = first[:, :, :up_piece]
    grad_down_inner = from_wire(first[:, :, up_piece:], local_blocks)
    preact = jnp.einsum("tjg,gjk->tkg", up_mixed, up_right, preferred_element_type=jnp.float32)
    sigmoid_val = jax.nn.sigmoid(preact)
    activated = (
        (preact * sigmoid_val)
        .reshape(tok_rows, blocks_all, tiles_up, TILE_UP)
        .transpose(0, 2, 1, 3)
    )
    hidden = activated.reshape(tok_rows, local_blocks, hidden_width).astype(jnp.bfloat16)
    down_inner = jnp.einsum(
        "tbh,bhc->tbc", hidden, down_full, preferred_element_type=jnp.float32
    ).astype(jnp.bfloat16)
    grad_hidden = jnp.einsum(
        "tbc,bhc->tbh", grad_down_inner, down_full, preferred_element_type=jnp.float32
    )
    grad_hidden = grad_hidden.reshape(tok_rows, tiles_up, blocks_all, TILE_UP).transpose(0, 2, 1, 3)
    grad_hidden = grad_hidden.reshape(tok_rows, blocks_all, group_up)
    grad_preact = (grad_hidden * sigmoid_val * (1.0 + preact * (1.0 - sigmoid_val))).astype(
        jnp.bfloat16
    )
    grad_up_mixed = jnp.einsum(
        "tkg,gjk->tjg", grad_preact, up_right, preferred_element_type=jnp.float32
    ).astype(jnp.bfloat16)
    right_up_term = (
        jnp.einsum("tjg,tkg->gjk", up_mixed, grad_preact, preferred_element_type=jnp.float32)
        * grad_scale
    )
    down_part = jnp.einsum(
        "tbh,tbc->hbc", hidden, grad_down_inner, preferred_element_type=jnp.float32
    )
    down_piece = block_width // feat_count
    second = exchange(
        jnp.concatenate([to_wire(down_inner, feat_count), grad_up_mixed], axis=2)
    )
    down_mixed = second[:, :, :down_piece].reshape(tok_rows, blocks_all * group_down)
    grad_up_inner = from_wire(second[:, :, down_piece:], local_blocks)
    layer_out = jnp.dot(down_mixed, mix_matrix, preferred_element_type=jnp.float32).astype(
        jnp.bfloat16
    )
    grad_by_group = layer_grad.reshape(tok_rows, tiles_down, blocks_all, TILE_DOWN).transpose(
        0, 2, 1, 3
    )
    grad_by_group = grad_by_group.reshape(tok_rows, blocks_all, group_down)
    right_down_term = (
        jnp.einsum(
            "tjc,tkc->cjk",
            down_mixed.reshape(tok_rows, blocks_all, group_down),
            grad_by_group,
            preferred_element_type=jnp.float32,
        )
        * grad_scale
    )
    grad_tokens = jnp.einsum(
        "tbg,big->tbi", grad_up_inner, up_full, preferred_element_type=jnp.float32
    ).astype(jnp.bfloat16)
    grad_tokens = grad_tokens.reshape(tok_rows, local_blocks * block_width)
    up_part = jnp.einsum(
        "tbi,tbg->ibg", token_blocks, grad_up_inner, preferred_element_type=jnp.float32
    )
    n_rows = up_part.shape[0] // up_rows
    parts = jnp.stack(
        [
            up_part.reshape(n_rows, up_rows, hidden_width),
            down_part.reshape(n_rows, up_rows, hidden_width),
        ],
        axis=1,
    )
    summed = dp_reduce_scatter(parts * grad_scale)[0]
    grad_up_left = summed[0][None]
    grad_down_left = summed[1].reshape(1, hidden_rows, block_width)
    rights = jnp.concatenate([right_up_term, right_down_term], axis=0)
    rights = dp_all_reduce(rights)
    grad_up_right = rights[:group_up]
    grad_down_right = rights[group_up:]
    return (layer_out, grad_tokens, grad_up_left, grad_up_right, grad_down_left, grad_down_right)


def solution(mesh):
    fine = split_mesh(mesh)
    row = P(DP_AXES, FEAT_AXES)
    weight = P(FEAT_AXES, DP_AXES, None)
    mixer = P(FEAT_AXES, None, None)
    return jax.shard_map(
        on_device,
        mesh=fine,
        in_specs=(row, weight, mixer, weight, mixer, row),
        out_specs=(row, row, weight, mixer, weight, mixer),
        check_vma=False,
    )
```

```python
import jax
import jax.numpy as jnp
import numpy as np
from jax import lax
from jax.sharding import Mesh
from jax.sharding import PartitionSpec as P

TILE_UP = 128
TILE_DOWN = 32

DP_AXES = ("z", "ylo", "core")
FEAT_AXES = ("yhi", "x")


def split_mesh(mesh):
    n_dp = mesh.shape["dp"]
    n_feat = mesh.shape["feat"]
    sizes = (n_dp // 4, 2, 2, n_feat // 4, 4)
    devices = np.asarray(mesh.devices).reshape(sizes)
    return Mesh(devices, DP_AXES + FEAT_AXES)


def exchange(wired):
    rows, feat_count, piece = wired.shape
    n_x = lax.axis_size("x")
    n_y = feat_count // n_x
    shaped = wired.reshape(rows, n_y, n_x, piece)
    shaped = lax.all_to_all(shaped, "x", 2, 2, tiled=True)
    shaped = lax.all_to_all(shaped, "yhi", 1, 1, tiled=True)
    return shaped.reshape(rows, feat_count, piece)


def shift(value, axis, step):
    n = lax.axis_size(axis)
    return lax.ppermute(value, axis, [(i, (i + step) % n) for i in range(n)])


def swap(value, axis, mask):
    n = lax.axis_size(axis)
    return lax.ppermute(value, axis, [(i, i ^ mask) for i in range(n)])


def z_ring_reduce_scatter(x):
    n = x.shape[0]
    me = lax.axis_index("z")
    n_fwd = n // 2
    n_bwd = n - 1 - n_fwd
    fwd = None
    bwd = None
    for step in range(1, n_fwd + 1):
        own = lax.dynamic_index_in_dim(x, (me + n_fwd + 1 - step) % n, 0, keepdims=False)
        fwd = shift(own if fwd is None else fwd + own, "z", 1)
        if step <= n_bwd:
            own = lax.dynamic_index_in_dim(x, (me - n_bwd - 1 + step) % n, 0, keepdims=False)
            bwd = shift(own if bwd is None else bwd + own, "z", -1)
    return fwd + bwd + lax.dynamic_index_in_dim(x, me, 0, keepdims=False)


def z_ring_all_gather(chunk):
    n = lax.axis_size("z")
    me = lax.axis_index("z")
    out = jnp.zeros((n,) + chunk.shape, chunk.dtype)
    out = lax.dynamic_update_index_in_dim(out, chunk, me, 0)
    fwd = chunk
    bwd = chunk
    n_fwd = n // 2
    for step in range(1, n_fwd + 1):
        fwd = shift(fwd, "z", 1)
        out = lax.dynamic_update_index_in_dim(out, fwd, (me - step) % n, 0)
        if step < n - n_fwd:
            bwd = shift(bwd, "z", -1)
            out = lax.dynamic_update_index_in_dim(out, bwd, (me + step) % n, 0)
    return out


def swap_with(value, extra, axis):
    flat = jnp.concatenate([value.reshape(-1), extra.reshape(-1)])
    got = swap(flat, axis, 1)
    return got[: value.size].reshape(value.shape), got[value.size :].reshape(extra.shape)


def dp_reduce_scatter(part, small):
    rows = part.shape[0]
    rest = part.shape[1:]
    n_z = lax.axis_size("z")
    x = part.reshape((n_z, 2, 2, rows // (4 * n_z)) + rest)
    core = lax.axis_index("core")
    mine = lax.dynamic_index_in_dim(x, core, 2, keepdims=False)
    other = lax.dynamic_index_in_dim(x, 1 - core, 2, keepdims=False)
    got, got_small = swap_with(other, small, "core")
    x = mine + got
    small = small + got_small
    mask = 1
    while mask < n_z:
        small = small + swap(small, "z", mask)
        mask *= 2
    x = z_ring_reduce_scatter(x)
    ylo = lax.axis_index("ylo")
    mine = lax.dynamic_index_in_dim(x, ylo, 0, keepdims=False)
    other = lax.dynamic_index_in_dim(x, 1 - ylo, 0, keepdims=False)
    got, got_small = swap_with(other, small, "ylo")
    return mine + got, small + got_small


def dp_all_gather(local):
    ylo = lax.axis_index("ylo")
    got = swap(local, "ylo", 1)
    pair = jnp.where(ylo == 0, jnp.stack([local, got]), jnp.stack([got, local]))
    ring = z_ring_all_gather(pair)
    core = lax.axis_index("core")
    other = swap(ring, "core", 1)
    both = jnp.where(core == 0, jnp.stack([ring, other], 2), jnp.stack([other, ring], 2))
    return both.reshape((-1,) + local.shape[1:])


def to_wire(blocks, feat_count):
    tok_rows, local_blocks, full_width = blocks.shape
    piece = full_width // feat_count
    shaped = blocks.reshape(tok_rows, local_blocks, feat_count, piece).transpose(0, 2, 1, 3)
    return shaped.reshape(tok_rows, feat_count, local_blocks * piece)


def from_wire(wired, local_blocks):
    tok_rows, feat_count, line_len = wired.shape
    piece = line_len // local_blocks
    shaped = wired.reshape(tok_rows, feat_count, local_blocks, piece).transpose(0, 2, 1, 3)
    return shaped.reshape(tok_rows, local_blocks, feat_count * piece)


def on_device(tokens, up_left, up_right, down_left, down_right, layer_grad):
    tok_rows = tokens.shape[0]
    local_blocks = up_left.shape[0]
    hidden_width = up_left.shape[2]
    block_width = down_left.shape[2]
    blocks_all = up_right.shape[1]
    group_up = up_right.shape[0]
    group_down = down_right.shape[0]
    feat_count = lax.axis_size("yhi") * lax.axis_size("x")
    n_dp = lax.axis_size("z") * lax.axis_size("ylo") * lax.axis_size("core")
    grad_scale = float(tok_rows * n_dp) ** (-0.5)
    tiles_up = group_up // TILE_UP
    tiles_down = group_down // TILE_DOWN
    hidden_rows = down_left.shape[1]
    up_rows = up_left.shape[1]
    weights = jnp.concatenate(
        [up_left[0], down_left[0].reshape(up_rows, hidden_rows * block_width // up_rows)], axis=1
    )
    weights = dp_all_gather(weights)
    up_full = weights[:, :hidden_width][None]
    down_full = weights[:, hidden_width:].reshape(1, -1, block_width)
    token_blocks = tokens.reshape(tok_rows, local_blocks, block_width)
    identity = jnp.eye(group_down, dtype=jnp.bfloat16).reshape(group_down, tiles_down, TILE_DOWN)
    mix_matrix = jnp.einsum(
        "cjk,cal->jcakl", down_right, identity, preferred_element_type=jnp.float32
    )
    mix_matrix = mix_matrix.astype(jnp.bfloat16).reshape(
        blocks_all * group_down, blocks_all * group_down
    )
    grad_down_mixed = lax.dot_general(
        layer_grad, mix_matrix, (((1,), (1,)), ((), ())), preferred_element_type=jnp.float32
    ).astype(jnp.bfloat16)
    up_inner = jnp.einsum(
        "tbi,big->tbg", token_blocks, up_full, preferred_element_type=jnp.float32
    ).astype(jnp.bfloat16)
    up_piece = hidden_width // feat_count
    first = exchange(
        jnp.concatenate(
            [
                to_wire(up_inner, feat_count),
                grad_down_mixed.reshape(tok_rows, feat_count, local_blocks * group_down),
            ],
            axis=2,
        )
    )
    up_mixed = first[:, :, :up_piece]
    grad_down_inner = from_wire(first[:, :, up_piece:], local_blocks)
    preact = jnp.einsum("tjg,gjk->tkg", up_mixed, up_right, preferred_element_type=jnp.float32)
    sigmoid_val = jax.nn.sigmoid(preact)
    activated = (
        (preact * sigmoid_val)
        .reshape(tok_rows, blocks_all, tiles_up, TILE_UP)
        .transpose(0, 2, 1, 3)
    )
    hidden = activated.reshape(tok_rows, local_blocks, hidden_width).astype(jnp.bfloat16)
    down_inner = jnp.einsum(
        "tbh,bhc->tbc", hidden, down_full, preferred_element_type=jnp.float32
    ).astype(jnp.bfloat16)
    grad_hidden = jnp.einsum(
        "tbc,bhc->tbh", grad_down_inner, down_full, preferred_element_type=jnp.float32
    )
    grad_hidden = grad_hidden.reshape(tok_rows, tiles_up, blocks_all, TILE_UP).transpose(0, 2, 1, 3)
    grad_hidden = grad_hidden.reshape(tok_rows, blocks_all, group_up)
    grad_preact = (grad_hidden * sigmoid_val * (1.0 + preact * (1.0 - sigmoid_val))).astype(
        jnp.bfloat16
    )
    grad_up_mixed = jnp.einsum(
        "tkg,gjk->tjg", grad_preact, up_right, preferred_element_type=jnp.float32
    ).astype(jnp.bfloat16)
    right_up_term = (
        jnp.einsum("tjg,tkg->gjk", up_mixed, grad_preact, preferred_element_type=jnp.float32)
        * grad_scale
    )
    down_part = jnp.einsum(
        "tbh,tbc->hbc", hidden, grad_down_inner, preferred_element_type=jnp.float32
    )
    down_piece = block_width // feat_count
    second = exchange(
        jnp.concatenate([to_wire(down_inner, feat_count), grad_up_mixed], axis=2)
    )
    down_mixed = second[:, :, :down_piece].reshape(tok_rows, blocks_all * group_down)
    grad_up_inner = from_wire(second[:, :, down_piece:], local_blocks)
    layer_out = jnp.dot(down_mixed, mix_matrix, preferred_element_type=jnp.float32).astype(
        jnp.bfloat16
    )
    grad_by_group = layer_grad.reshape(tok_rows, tiles_down, blocks_all, TILE_DOWN).transpose(
        0, 2, 1, 3
    )
    grad_by_group = grad_by_group.reshape(tok_rows, blocks_all, group_down)
    right_down_term = (
        jnp.einsum(
            "tjc,tkc->cjk",
            down_mixed.reshape(tok_rows, blocks_all, group_down),
            grad_by_group,
            preferred_element_type=jnp.float32,
        )
        * grad_scale
    )
    grad_tokens = jnp.einsum(
        "tbg,big->tbi", grad_up_inner, up_full, preferred_element_type=jnp.float32
    ).astype(jnp.bfloat16)
    grad_tokens = grad_tokens.reshape(tok_rows, local_blocks * block_width)
    up_part = jnp.einsum(
        "tbi,tbg->ibg", token_blocks, grad_up_inner, preferred_element_type=jnp.float32
    )
    n_rows = up_part.shape[0] // up_rows
    parts = jnp.stack(
        [
            up_part.reshape(n_rows, up_rows, hidden_width),
            down_part.reshape(n_rows, up_rows, hidden_width),
        ],
        axis=1,
    )
    rights = jnp.concatenate([right_up_term, right_down_term], axis=0)
    summed, rights = dp_reduce_scatter(parts * grad_scale, rights)
    summed = summed[0]
    grad_up_left = summed[0][None]
    grad_down_left = summed[1].reshape(1, hidden_rows, block_width)
    grad_up_right = rights[:group_up]
    grad_down_right = rights[group_up:]
    return (layer_out, grad_tokens, grad_up_left, grad_up_right, grad_down_left, grad_down_right)


def solution(mesh):
    fine = split_mesh(mesh)
    row = P(DP_AXES, FEAT_AXES)
    weight = P(FEAT_AXES, DP_AXES, None)
    mixer = P(FEAT_AXES, None, None)
    return jax.shard_map(
        on_device,
        mesh=fine,
        in_specs=(row, weight, mixer, weight, mixer, row),
        out_specs=(row, row, weight, mixer, weight, mixer),
        check_vma=False,
    )
```

```python
import jax
import jax.numpy as jnp
import numpy as np
from jax import lax
from jax.sharding import Mesh
from jax.sharding import PartitionSpec as P

TILE_UP = 128
TILE_DOWN = 32

DP_AXES = ("z", "ylo", "core")
FEAT_AXES = ("yhi", "x")


def split_mesh(mesh):
    n_dp = mesh.shape["dp"]
    n_feat = mesh.shape["feat"]
    sizes = (n_dp // 4, 2, 2, n_feat // 4, 4)
    devices = np.asarray(mesh.devices).reshape(sizes)
    return Mesh(devices, DP_AXES + FEAT_AXES)


def exchange(wired):
    return lax.all_to_all(wired, FEAT_AXES, 1, 1, tiled=True)


def shift(value, axis, step):
    n = lax.axis_size(axis)
    return lax.ppermute(value, axis, [(i, (i + step) % n) for i in range(n)])


def swap(value, axis, mask):
    n = lax.axis_size(axis)
    return lax.ppermute(value, axis, [(i, i ^ mask) for i in range(n)])


def z_ring_reduce_scatter(x):
    n = x.shape[0]
    me = lax.axis_index("z")
    lo, hi = jnp.split(x, 2, axis=-1)
    fwd = None
    bwd = None
    for step in range(1, n):
        own_f = lax.dynamic_index_in_dim(lo, (me - step) % n, 0, keepdims=False)
        own_b = lax.dynamic_index_in_dim(hi, (me + step) % n, 0, keepdims=False)
        fwd = shift(own_f if fwd is None else fwd + own_f, "z", 1)
        bwd = shift(own_b if bwd is None else bwd + own_b, "z", -1)
    fwd = fwd + lax.dynamic_index_in_dim(lo, me, 0, keepdims=False)
    bwd = bwd + lax.dynamic_index_in_dim(hi, me, 0, keepdims=False)
    return jnp.concatenate([fwd, bwd], axis=-1)


def z_ring_all_gather(chunk):
    n = lax.axis_size("z")
    me = lax.axis_index("z")
    out = jnp.zeros((n,) + chunk.shape, chunk.dtype)
    out = lax.dynamic_update_index_in_dim(out, chunk, me, 0)
    fwd = chunk
    bwd = chunk
    half = n // 2
    for step in range(1, half):
        fwd = shift(fwd, "z", 1)
        bwd = shift(bwd, "z", -1)
        out = lax.dynamic_update_index_in_dim(out, fwd, (me - step) % n, 0)
        out = lax.dynamic_update_index_in_dim(out, bwd, (me + step) % n, 0)
    lo, _ = jnp.split(fwd, 2, axis=-1)
    _, hi = jnp.split(bwd, 2, axis=-1)
    last = jnp.concatenate([shift(lo, "z", 1), shift(hi, "z", -1)], axis=-1)
    out = lax.dynamic_update_index_in_dim(out, last, (me + half) % n, 0)
    return out


def dp_reduce_scatter(part):
    rows = part.shape[0]
    rest = part.shape[1:]
    n_z = lax.axis_size("z")
    x = part.reshape((n_z, 2, 2, rows // (4 * n_z)) + rest)
    core = lax.axis_index("core")
    mine = lax.dynamic_index_in_dim(x, core, 2, keepdims=False)
    other = lax.dynamic_index_in_dim(x, 1 - core, 2, keepdims=False)
    x = mine + swap(other, "core", 1)
    x = z_ring_reduce_scatter(x)
    ylo = lax.axis_index("ylo")
    mine = lax.dynamic_index_in_dim(x, ylo, 0, keepdims=False)
    other = lax.dynamic_index_in_dim(x, 1 - ylo, 0, keepdims=False)
    return mine + swap(other, "ylo", 1)


def dp_all_gather(local):
    ylo = lax.axis_index("ylo")
    got = swap(local, "ylo", 1)
    pair = jnp.where(ylo == 0, jnp.stack([local, got]), jnp.stack([got, local]))
    ring = z_ring_all_gather(pair)
    core = lax.axis_index("core")
    other = swap(ring, "core", 1)
    both = jnp.where(core == 0, jnp.stack([ring, other], 2), jnp.stack([other, ring], 2))
    return both.reshape((-1,) + local.shape[1:])


def dp_all_reduce(x):
    x = x + swap(x, "core", 1)
    x = x + swap(x, "ylo", 1)
    mask = 1
    while mask < lax.axis_size("z"):
        x = x + swap(x, "z", mask)
        mask *= 2
    return x


def to_wire(blocks, feat_count):
    tok_rows, local_blocks, full_width = blocks.shape
    piece = full_width // feat_count
    shaped = blocks.reshape(tok_rows, local_blocks, feat_count, piece).transpose(0, 2, 1, 3)
    return shaped.reshape(tok_rows, feat_count, local_blocks * piece)


def from_wire(wired, local_blocks):
    tok_rows, feat_count, line_len = wired.shape
    piece = line_len // local_blocks
    shaped = wired.reshape(tok_rows, feat_count, local_blocks, piece).transpose(0, 2, 1, 3)
    return shaped.reshape(tok_rows, local_blocks, feat_count * piece)


def on_device(tokens, up_left, up_right, down_left, down_right, layer_grad):
    tok_rows = tokens.shape[0]
    local_blocks = up_left.shape[0]
    hidden_width = up_left.shape[2]
    block_width = down_left.shape[2]
    blocks_all = up_right.shape[1]
    group_up = up_right.shape[0]
    group_down = down_right.shape[0]
    feat_count = lax.axis_size("yhi") * lax.axis_size("x")
    n_dp = lax.axis_size("z") * lax.axis_size("ylo") * lax.axis_size("core")
    grad_scale = float(tok_rows * n_dp) ** (-0.5)
    tiles_up = group_up // TILE_UP
    tiles_down = group_down // TILE_DOWN
    hidden_rows = down_left.shape[1]
    up_rows = up_left.shape[1]
    weights = jnp.concatenate(
        [up_left[0], down_left[0].reshape(up_rows, hidden_rows * block_width // up_rows)], axis=1
    )
    weights = dp_all_gather(weights)
    up_full = weights[:, :hidden_width][None]
    down_full = weights[:, hidden_width:].reshape(1, -1, block_width)
    token_blocks = tokens.reshape(tok_rows, local_blocks, block_width)
    identity = jnp.eye(group_down, dtype=jnp.bfloat16).reshape(group_down, tiles_down, TILE_DOWN)
    mix_matrix = jnp.einsum(
        "cjk,cal->jcakl", down_right, identity, preferred_element_type=jnp.float32
    )
    mix_matrix = mix_matrix.astype(jnp.bfloat16).reshape(
        blocks_all * group_down, blocks_all * group_down
    )
    grad_down_mixed = lax.dot_general(
        layer_grad, mix_matrix, (((1,), (1,)), ((), ())), preferred_element_type=jnp.float32
    ).astype(jnp.bfloat16)
    up_inner = jnp.einsum(
        "tbi,big->tbg", token_blocks, up_full, preferred_element_type=jnp.float32
    ).astype(jnp.bfloat16)
    up_piece = hidden_width // feat_count
    first = exchange(
        jnp.concatenate(
            [
                to_wire(up_inner, feat_count),
                grad_down_mixed.reshape(tok_rows, feat_count, local_blocks * group_down),
            ],
            axis=2,
        )
    )
    up_mixed = first[:, :, :up_piece]
    grad_down_inner = from_wire(first[:, :, up_piece:], local_blocks)
    preact = jnp.einsum("tjg,gjk->tkg", up_mixed, up_right, preferred_element_type=jnp.float32)
    sigmoid_val = jax.nn.sigmoid(preact)
    activated = (
        (preact * sigmoid_val)
        .reshape(tok_rows, blocks_all, tiles_up, TILE_UP)
        .transpose(0, 2, 1, 3)
    )
    hidden = activated.reshape(tok_rows, local_blocks, hidden_width).astype(jnp.bfloat16)
    down_inner = jnp.einsum(
        "tbh,bhc->tbc", hidden, down_full, preferred_element_type=jnp.float32
    ).astype(jnp.bfloat16)
    grad_hidden = jnp.einsum(
        "tbc,bhc->tbh", grad_down_inner, down_full, preferred_element_type=jnp.float32
    )
    grad_hidden = grad_hidden.reshape(tok_rows, tiles_up, blocks_all, TILE_UP).transpose(0, 2, 1, 3)
    grad_hidden = grad_hidden.reshape(tok_rows, blocks_all, group_up)
    grad_preact = (grad_hidden * sigmoid_val * (1.0 + preact * (1.0 - sigmoid_val))).astype(
        jnp.bfloat16
    )
    grad_up_mixed = jnp.einsum(
        "tkg,gjk->tjg", grad_preact, up_right, preferred_element_type=jnp.float32
    ).astype(jnp.bfloat16)
    right_up_term = (
        jnp.einsum("tjg,tkg->gjk", up_mixed, grad_preact, preferred_element_type=jnp.float32)
        * grad_scale
    )
    down_part = jnp.einsum(
        "tbh,tbc->hbc", hidden, grad_down_inner, preferred_element_type=jnp.float32
    )
    down_piece = block_width // feat_count
    second = exchange(
        jnp.concatenate([to_wire(down_inner, feat_count), grad_up_mixed], axis=2)
    )
    down_mixed = second[:, :, :down_piece].reshape(tok_rows, blocks_all * group_down)
    grad_up_inner = from_wire(second[:, :, down_piece:], local_blocks)
    layer_out = jnp.dot(down_mixed, mix_matrix, preferred_element_type=jnp.float32).astype(
        jnp.bfloat16
    )
    grad_by_group = layer_grad.reshape(tok_rows, tiles_down, blocks_all, TILE_DOWN).transpose(
        0, 2, 1, 3
    )
    grad_by_group = grad_by_group.reshape(tok_rows, blocks_all, group_down)
    right_down_term = (
        jnp.einsum(
            "tjc,tkc->cjk",
            down_mixed.reshape(tok_rows, blocks_all, group_down),
            grad_by_group,
            preferred_element_type=jnp.float32,
        )
        * grad_scale
    )
    grad_tokens = jnp.einsum(
        "tbg,big->tbi", grad_up_inner, up_full, preferred_element_type=jnp.float32
    ).astype(jnp.bfloat16)
    grad_tokens = grad_tokens.reshape(tok_rows, local_blocks * block_width)
    up_part = jnp.einsum(
        "tbi,tbg->ibg", token_blocks, grad_up_inner, preferred_element_type=jnp.float32
    )
    n_rows = up_part.shape[0] // up_rows
    parts = jnp.stack(
        [
            up_part.reshape(n_rows, up_rows, hidden_width),
            down_part.reshape(n_rows, up_rows, hidden_width),
        ],
        axis=1,
    )
    summed = dp_reduce_scatter(parts * grad_scale)[0]
    grad_up_left = summed[0][None]
    grad_down_left = summed[1].reshape(1, hidden_rows, block_width)
    rights = jnp.concatenate([right_up_term, right_down_term], axis=0)
    rights = dp_all_reduce(rights)
    grad_up_right = rights[:group_up]
    grad_down_right = rights[group_up:]
    return (layer_out, grad_tokens, grad_up_left, grad_up_right, grad_down_left, grad_down_right)


def solution(mesh):
    fine = split_mesh(mesh)
    row = P(DP_AXES, FEAT_AXES)
    weight = P(FEAT_AXES, DP_AXES, None)
    mixer = P(FEAT_AXES, None, None)
    return jax.shard_map(
        on_device,
        mesh=fine,
        in_specs=(row, weight, mixer, weight, mixer, row),
        out_specs=(row, row, weight, mixer, weight, mixer),
        check_vma=False,
    )
```

```python
import jax
import jax.numpy as jnp
import numpy as np
from jax import lax
from jax.sharding import Mesh
from jax.sharding import PartitionSpec as P

TILE_UP = 128
TILE_DOWN = 32

DP_AXES = ("z", "ylo", "core")
FEAT_AXES = ("yhi", "x")


def split_mesh(mesh):
    n_dp = mesh.shape["dp"]
    n_feat = mesh.shape["feat"]
    sizes = (n_dp // 4, 2, 2, n_feat // 4, 4)
    devices = np.asarray(mesh.devices).reshape(sizes)
    return Mesh(devices, DP_AXES + FEAT_AXES)


def exchange(wired):
    return lax.all_to_all(wired, FEAT_AXES, 1, 1, tiled=True)


def shift(value, axis, step):
    n = lax.axis_size(axis)
    return lax.ppermute(value, axis, [(i, (i + step) % n) for i in range(n)])


def swap(value, axis, mask):
    n = lax.axis_size(axis)
    return lax.ppermute(value, axis, [(i, i ^ mask) for i in range(n)])


def z_ring_reduce_scatter(x):
    n = x.shape[0]
    me = lax.axis_index("z")
    lo, hi = jnp.split(x, 2, axis=-1)
    fwd = None
    bwd = None
    for step in range(1, n):
        own_f = lax.dynamic_index_in_dim(lo, (me - step) % n, 0, keepdims=False)
        own_b = lax.dynamic_index_in_dim(hi, (me + step) % n, 0, keepdims=False)
        fwd = shift(own_f if fwd is None else fwd + own_f, "z", 1)
        bwd = shift(own_b if bwd is None else bwd + own_b, "z", -1)
    fwd = fwd + lax.dynamic_index_in_dim(lo, me, 0, keepdims=False)
    bwd = bwd + lax.dynamic_index_in_dim(hi, me, 0, keepdims=False)
    return jnp.concatenate([fwd, bwd], axis=-1)


def z_ring_all_gather(chunk):
    n = lax.axis_size("z")
    me = lax.axis_index("z")
    out = jnp.zeros((n,) + chunk.shape, chunk.dtype)
    out = lax.dynamic_update_index_in_dim(out, chunk, me, 0)
    fwd = chunk
    bwd = chunk
    half = n // 2
    for step in range(1, half):
        fwd = shift(fwd, "z", 1)
        bwd = shift(bwd, "z", -1)
        out = lax.dynamic_update_index_in_dim(out, fwd, (me - step) % n, 0)
        out = lax.dynamic_update_index_in_dim(out, bwd, (me + step) % n, 0)
    lo, _ = jnp.split(fwd, 2, axis=-1)
    _, hi = jnp.split(bwd, 2, axis=-1)
    last = jnp.concatenate([shift(lo, "z", 1), shift(hi, "z", -1)], axis=-1)
    out = lax.dynamic_update_index_in_dim(out, last, (me + half) % n, 0)
    return out


def dp_reduce_scatter(part):
    rows = part.shape[0]
    rest = part.shape[1:]
    n_z = lax.axis_size("z")
    x = part.reshape((n_z, 2, 2, rows // (4 * n_z)) + rest)
    core = lax.axis_index("core")
    mine = lax.dynamic_index_in_dim(x, core, 2, keepdims=False)
    other = lax.dynamic_index_in_dim(x, 1 - core, 2, keepdims=False)
    x = mine + swap(other, "core", 1)
    x = z_ring_reduce_scatter(x)
    ylo = lax.axis_index("ylo")
    mine = lax.dynamic_index_in_dim(x, ylo, 0, keepdims=False)
    other = lax.dynamic_index_in_dim(x, 1 - ylo, 0, keepdims=False)
    return mine + swap(other, "ylo", 1)


def sc_reduce_scatter(part):
    rows = part.shape[0]
    rest = part.shape[1:]
    n_zy = lax.axis_size("z") * lax.axis_size("ylo")
    x = part.reshape((n_zy, 2, rows // (2 * n_zy)) + rest)
    core = lax.axis_index("core")
    mine = lax.dynamic_index_in_dim(x, core, 1, keepdims=False)
    other = lax.dynamic_index_in_dim(x, 1 - core, 1, keepdims=False)
    x = mine + swap(other, "core", 1)
    x = lax.psum_scatter(x, ("z", "ylo"), scatter_dimension=0, tiled=True)
    return x.reshape((rows // (2 * n_zy),) + rest)


def dp_all_gather(local):
    ylo = lax.axis_index("ylo")
    got = swap(local, "ylo", 1)
    pair = jnp.where(ylo == 0, jnp.stack([local, got]), jnp.stack([got, local]))
    ring = z_ring_all_gather(pair)
    core = lax.axis_index("core")
    other = swap(ring, "core", 1)
    both = jnp.where(core == 0, jnp.stack([ring, other], 2), jnp.stack([other, ring], 2))
    return both.reshape((-1,) + local.shape[1:])


def dp_all_reduce(x):
    x = x + swap(x, "core", 1)
    x = x + swap(x, "ylo", 1)
    mask = 1
    while mask < lax.axis_size("z"):
        x = x + swap(x, "z", mask)
        mask *= 2
    return x


def to_wire(blocks, feat_count):
    tok_rows, local_blocks, full_width = blocks.shape
    piece = full_width // feat_count
    shaped = blocks.reshape(tok_rows, local_blocks, feat_count, piece).transpose(0, 2, 1, 3)
    return shaped.reshape(tok_rows, feat_count, local_blocks * piece)


def from_wire(wired, local_blocks):
    tok_rows, feat_count, line_len = wired.shape
    piece = line_len // local_blocks
    shaped = wired.reshape(tok_rows, feat_count, local_blocks, piece).transpose(0, 2, 1, 3)
    return shaped.reshape(tok_rows, local_blocks, feat_count * piece)


def on_device(tokens, up_left, up_right, down_left, down_right, layer_grad):
    tok_rows = tokens.shape[0]
    local_blocks = up_left.shape[0]
    hidden_width = up_left.shape[2]
    block_width = down_left.shape[2]
    blocks_all = up_right.shape[1]
    group_up = up_right.shape[0]
    group_down = down_right.shape[0]
    feat_count = lax.axis_size("yhi") * lax.axis_size("x")
    n_dp = lax.axis_size("z") * lax.axis_size("ylo") * lax.axis_size("core")
    grad_scale = float(tok_rows * n_dp) ** (-0.5)
    tiles_up = group_up // TILE_UP
    tiles_down = group_down // TILE_DOWN
    down_full = lax.all_gather(down_left, DP_AXES, axis=1, tiled=True)
    up_full = dp_all_gather(up_left[0])[None]
    token_blocks = tokens.reshape(tok_rows, local_blocks, block_width)
    identity = jnp.eye(group_down, dtype=jnp.bfloat16).reshape(group_down, tiles_down, TILE_DOWN)
    mix_matrix = jnp.einsum(
        "cjk,cal->jcakl", down_right, identity, preferred_element_type=jnp.float32
    )
    mix_matrix = mix_matrix.astype(jnp.bfloat16).reshape(
        blocks_all * group_down, blocks_all * group_down
    )
    grad_down_mixed = lax.dot_general(
        layer_grad, mix_matrix, (((1,), (1,)), ((), ())), preferred_element_type=jnp.float32
    ).astype(jnp.bfloat16)
    up_inner = jnp.einsum(
        "tbi,big->tbg", token_blocks, up_full, preferred_element_type=jnp.float32
    ).astype(jnp.bfloat16)
    up_piece = hidden_width // feat_count
    first = exchange(
        jnp.concatenate(
            [
                to_wire(up_inner, feat_count),
                grad_down_mixed.reshape(tok_rows, feat_count, local_blocks * group_down),
            ],
            axis=2,
        )
    )
    up_mixed = first[:, :, :up_piece]
    grad_down_inner = from_wire(first[:, :, up_piece:], local_blocks)
    preact = jnp.einsum("tjg,gjk->tkg", up_mixed, up_right, preferred_element_type=jnp.float32)
    sigmoid_val = jax.nn.sigmoid(preact)
    activated = (
        (preact * sigmoid_val)
        .reshape(tok_rows, blocks_all, tiles_up, TILE_UP)
        .transpose(0, 2, 1, 3)
    )
    hidden = activated.reshape(tok_rows, local_blocks, hidden_width).astype(jnp.bfloat16)
    down_inner = jnp.einsum(
        "tbh,bhc->tbc", hidden, down_full, preferred_element_type=jnp.float32
    ).astype(jnp.bfloat16)
    grad_hidden = jnp.einsum(
        "tbc,bhc->tbh", grad_down_inner, down_full, preferred_element_type=jnp.float32
    )
    grad_hidden = grad_hidden.reshape(tok_rows, tiles_up, blocks_all, TILE_UP).transpose(0, 2, 1, 3)
    grad_hidden = grad_hidden.reshape(tok_rows, blocks_all, group_up)
    grad_preact = (grad_hidden * sigmoid_val * (1.0 + preact * (1.0 - sigmoid_val))).astype(
        jnp.bfloat16
    )
    grad_up_mixed = jnp.einsum(
        "tkg,gjk->tjg", grad_preact, up_right, preferred_element_type=jnp.float32
    ).astype(jnp.bfloat16)
    right_up_term = (
        jnp.einsum("tjg,tkg->gjk", up_mixed, grad_preact, preferred_element_type=jnp.float32)
        * grad_scale
    )
    down_part = jnp.einsum(
        "tbh,tbc->hbc", hidden, grad_down_inner, preferred_element_type=jnp.float32
    )
    grad_down_left = sc_reduce_scatter(down_part * grad_scale).transpose(1, 0, 2)
    down_piece = block_width // feat_count
    second = exchange(
        jnp.concatenate([to_wire(down_inner, feat_count), grad_up_mixed], axis=2)
    )
    down_mixed = second[:, :, :down_piece].reshape(tok_rows, blocks_all * group_down)
    grad_up_inner = from_wire(second[:, :, down_piece:], local_blocks)
    layer_out = jnp.dot(down_mixed, mix_matrix, preferred_element_type=jnp.float32).astype(
        jnp.bfloat16
    )
    grad_by_group = layer_grad.reshape(tok_rows, tiles_down, blocks_all, TILE_DOWN).transpose(
        0, 2, 1, 3
    )
    grad_by_group = grad_by_group.reshape(tok_rows, blocks_all, group_down)
    right_down_term = (
        jnp.einsum(
            "tjc,tkc->cjk",
            down_mixed.reshape(tok_rows, blocks_all, group_down),
            grad_by_group,
            preferred_element_type=jnp.float32,
        )
        * grad_scale
    )
    grad_tokens = jnp.einsum(
        "tbg,big->tbi", grad_up_inner, up_full, preferred_element_type=jnp.float32
    ).astype(jnp.bfloat16)
    grad_tokens = grad_tokens.reshape(tok_rows, local_blocks * block_width)
    up_part = jnp.einsum(
        "tbi,tbg->ibg", token_blocks, grad_up_inner, preferred_element_type=jnp.float32
    )
    grad_up_left = dp_reduce_scatter(up_part * grad_scale).transpose(1, 0, 2)
    rights = jnp.concatenate([right_up_term, right_down_term], axis=0)
    rights = dp_all_reduce(rights)
    grad_up_right = rights[:group_up]
    grad_down_right = rights[group_up:]
    return (layer_out, grad_tokens, grad_up_left, grad_up_right, grad_down_left, grad_down_right)


def solution(mesh):
    fine = split_mesh(mesh)
    row = P(DP_AXES, FEAT_AXES)
    weight = P(FEAT_AXES, DP_AXES, None)
    mixer = P(FEAT_AXES, None, None)
    return jax.shard_map(
        on_device,
        mesh=fine,
        in_specs=(row, weight, mixer, weight, mixer, row),
        out_specs=(row, row, weight, mixer, weight, mixer),
        check_vma=False,
    )
```

```python
import jax
import jax.numpy as jnp
import numpy as np
from jax import lax
from jax.sharding import Mesh
from jax.sharding import PartitionSpec as P

TILE_UP = 128
TILE_DOWN = 32

DP_AXES = ("z", "ylo", "core")
FEAT_AXES = ("yhi", "x")


def split_mesh(mesh):
    n_dp = mesh.shape["dp"]
    n_feat = mesh.shape["feat"]
    sizes = (n_dp // 4, 2, 2, n_feat // 4, 4)
    devices = np.asarray(mesh.devices).reshape(sizes)
    return Mesh(devices, DP_AXES + FEAT_AXES)


def exchange(wired):
    return lax.all_to_all(wired, FEAT_AXES, 1, 1, tiled=True)


def shift(value, axis, step):
    n = lax.axis_size(axis)
    return lax.ppermute(value, axis, [(i, (i + step) % n) for i in range(n)])


def swap(value, axis, mask):
    n = lax.axis_size(axis)
    return lax.ppermute(value, axis, [(i, i ^ mask) for i in range(n)])


def z_ring_reduce_scatter(x):
    n = x.shape[0]
    me = lax.axis_index("z")
    lo, hi = jnp.split(x, 2, axis=-1)
    fwd = None
    bwd = None
    for step in range(1, n):
        own_f = lax.dynamic_index_in_dim(lo, (me - step) % n, 0, keepdims=False)
        own_b = lax.dynamic_index_in_dim(hi, (me + step) % n, 0, keepdims=False)
        fwd = shift(own_f if fwd is None else fwd + own_f, "z", 1)
        bwd = shift(own_b if bwd is None else bwd + own_b, "z", -1)
    fwd = fwd + lax.dynamic_index_in_dim(lo, me, 0, keepdims=False)
    bwd = bwd + lax.dynamic_index_in_dim(hi, me, 0, keepdims=False)
    return jnp.concatenate([fwd, bwd], axis=-1)


def z_ring_all_gather(chunk):
    n = lax.axis_size("z")
    me = lax.axis_index("z")
    out = jnp.zeros((n,) + chunk.shape, chunk.dtype)
    out = lax.dynamic_update_index_in_dim(out, chunk, me, 0)
    fwd = chunk
    bwd = chunk
    half = n // 2
    for step in range(1, half):
        fwd = shift(fwd, "z", 1)
        bwd = shift(bwd, "z", -1)
        out = lax.dynamic_update_index_in_dim(out, fwd, (me - step) % n, 0)
        out = lax.dynamic_update_index_in_dim(out, bwd, (me + step) % n, 0)
    lo, _ = jnp.split(fwd, 2, axis=-1)
    _, hi = jnp.split(bwd, 2, axis=-1)
    last = jnp.concatenate([shift(lo, "z", 1), shift(hi, "z", -1)], axis=-1)
    out = lax.dynamic_update_index_in_dim(out, last, (me + half) % n, 0)
    return out


def dp_reduce_scatter(part):
    rows = part.shape[0]
    rest = part.shape[1:]
    n_z = lax.axis_size("z")
    x = part.reshape((n_z, 2, 2, rows // (4 * n_z)) + rest)
    core = lax.axis_index("core")
    mine = lax.dynamic_index_in_dim(x, core, 2, keepdims=False)
    other = lax.dynamic_index_in_dim(x, 1 - core, 2, keepdims=False)
    x = mine + swap(other, "core", 1)
    x = z_ring_reduce_scatter(x)
    ylo = lax.axis_index("ylo")
    mine = lax.dynamic_index_in_dim(x, ylo, 0, keepdims=False)
    other = lax.dynamic_index_in_dim(x, 1 - ylo, 0, keepdims=False)
    return mine + swap(other, "ylo", 1)


def dp_all_gather(local):
    ylo = lax.axis_index("ylo")
    got = swap(local, "ylo", 1)
    pair = jnp.where(ylo == 0, jnp.stack([local, got]), jnp.stack([got, local]))
    ring = z_ring_all_gather(pair)
    core = lax.axis_index("core")
    other = swap(ring, "core", 1)
    both = jnp.where(core == 0, jnp.stack([ring, other], 2), jnp.stack([other, ring], 2))
    return both.reshape((-1,) + local.shape[1:])


def dp_all_reduce(x):
    mask = lax.axis_size("z") // 2
    while mask >= 1:
        x = x + swap(x, "z", mask)
        mask //= 2
    x = x + swap(x, "ylo", 1)
    return x + swap(x, "core", 1)


def to_wire(blocks, feat_count):
    tok_rows, local_blocks, full_width = blocks.shape
    piece = full_width // feat_count
    shaped = blocks.reshape(tok_rows, local_blocks, feat_count, piece).transpose(0, 2, 1, 3)
    return shaped.reshape(tok_rows, feat_count, local_blocks * piece)


def from_wire(wired, local_blocks):
    tok_rows, feat_count, line_len = wired.shape
    piece = line_len // local_blocks
    shaped = wired.reshape(tok_rows, feat_count, local_blocks, piece).transpose(0, 2, 1, 3)
    return shaped.reshape(tok_rows, local_blocks, feat_count * piece)


def on_device(tokens, up_left, up_right, down_left, down_right, layer_grad):
    tok_rows = tokens.shape[0]
    local_blocks = up_left.shape[0]
    hidden_width = up_left.shape[2]
    block_width = down_left.shape[2]
    blocks_all = up_right.shape[1]
    group_up = up_right.shape[0]
    group_down = down_right.shape[0]
    feat_count = lax.axis_size("yhi") * lax.axis_size("x")
    n_dp = lax.axis_size("z") * lax.axis_size("ylo") * lax.axis_size("core")
    grad_scale = float(tok_rows * n_dp) ** (-0.5)
    tiles_up = group_up // TILE_UP
    tiles_down = group_down // TILE_DOWN
    hidden_rows = down_left.shape[1]
    up_rows = up_left.shape[1]
    weights = jnp.concatenate(
        [up_left[0], down_left[0].reshape(up_rows, hidden_rows * block_width // up_rows)], axis=1
    )
    weights = dp_all_gather(weights)
    up_full = weights[:, :hidden_width][None]
    down_full = weights[:, hidden_width:].reshape(1, -1, block_width)
    token_blocks = tokens.reshape(tok_rows, local_blocks, block_width)
    identity = jnp.eye(group_down, dtype=jnp.bfloat16).reshape(group_down, tiles_down, TILE_DOWN)
    mix_matrix = jnp.einsum(
        "cjk,cal->jcakl", down_right, identity, preferred_element_type=jnp.float32
    )
    mix_matrix = mix_matrix.astype(jnp.bfloat16).reshape(
        blocks_all * group_down, blocks_all * group_down
    )
    grad_down_mixed = lax.dot_general(
        layer_grad, mix_matrix, (((1,), (1,)), ((), ())), preferred_element_type=jnp.float32
    ).astype(jnp.bfloat16)
    up_inner = jnp.einsum(
        "tbi,big->tbg", token_blocks, up_full, preferred_element_type=jnp.float32
    ).astype(jnp.bfloat16)
    up_piece = hidden_width // feat_count
    first = exchange(
        jnp.concatenate(
            [
                to_wire(up_inner, feat_count),
                grad_down_mixed.reshape(tok_rows, feat_count, local_blocks * group_down),
            ],
            axis=2,
        )
    )
    up_mixed = first[:, :, :up_piece]
    grad_down_inner = from_wire(first[:, :, up_piece:], local_blocks)
    preact = jnp.einsum("tjg,gjk->tkg", up_mixed, up_right, preferred_element_type=jnp.float32)
    sigmoid_val = jax.nn.sigmoid(preact)
    activated = (
        (preact * sigmoid_val)
        .reshape(tok_rows, blocks_all, tiles_up, TILE_UP)
        .transpose(0, 2, 1, 3)
    )
    hidden = activated.reshape(tok_rows, local_blocks, hidden_width).astype(jnp.bfloat16)
    down_inner = jnp.einsum(
        "tbh,bhc->tbc", hidden, down_full, preferred_element_type=jnp.float32
    ).astype(jnp.bfloat16)
    grad_hidden = jnp.einsum(
        "tbc,bhc->tbh", grad_down_inner, down_full, preferred_element_type=jnp.float32
    )
    grad_hidden = grad_hidden.reshape(tok_rows, tiles_up, blocks_all, TILE_UP).transpose(0, 2, 1, 3)
    grad_hidden = grad_hidden.reshape(tok_rows, blocks_all, group_up)
    grad_preact = (grad_hidden * sigmoid_val * (1.0 + preact * (1.0 - sigmoid_val))).astype(
        jnp.bfloat16
    )
    grad_up_mixed = jnp.einsum(
        "tkg,gjk->tjg", grad_preact, up_right, preferred_element_type=jnp.float32
    ).astype(jnp.bfloat16)
    right_up_term = (
        jnp.einsum("tjg,tkg->gjk", up_mixed, grad_preact, preferred_element_type=jnp.float32)
        * grad_scale
    )
    down_part = jnp.einsum(
        "tbh,tbc->hbc", hidden, grad_down_inner, preferred_element_type=jnp.float32
    )
    down_piece = block_width // feat_count
    second = exchange(
        jnp.concatenate([to_wire(down_inner, feat_count), grad_up_mixed], axis=2)
    )
    down_mixed = second[:, :, :down_piece].reshape(tok_rows, blocks_all * group_down)
    grad_up_inner = from_wire(second[:, :, down_piece:], local_blocks)
    layer_out = jnp.dot(down_mixed, mix_matrix, preferred_element_type=jnp.float32).astype(
        jnp.bfloat16
    )
    grad_by_group = layer_grad.reshape(tok_rows, tiles_down, blocks_all, TILE_DOWN).transpose(
        0, 2, 1, 3
    )
    grad_by_group = grad_by_group.reshape(tok_rows, blocks_all, group_down)
    right_down_term = (
        jnp.einsum(
            "tjc,tkc->cjk",
            down_mixed.reshape(tok_rows, blocks_all, group_down),
            grad_by_group,
            preferred_element_type=jnp.float32,
        )
        * grad_scale
    )
    grad_tokens = jnp.einsum(
        "tbg,big->tbi", grad_up_inner, up_full, preferred_element_type=jnp.float32
    ).astype(jnp.bfloat16)
    grad_tokens = grad_tokens.reshape(tok_rows, local_blocks * block_width)
    up_part = jnp.einsum(
        "tbi,tbg->ibg", token_blocks, grad_up_inner, preferred_element_type=jnp.float32
    )
    n_rows = up_part.shape[0] // up_rows
    parts = jnp.stack(
        [
            up_part.reshape(n_rows, up_rows, hidden_width),
            down_part.reshape(n_rows, up_rows, hidden_width),
        ],
        axis=1,
    )
    summed = dp_reduce_scatter(parts * grad_scale)[0]
    grad_up_left = summed[0][None]
    grad_down_left = summed[1].reshape(1, hidden_rows, block_width)
    rights = jnp.concatenate([right_up_term, right_down_term], axis=0)
    rights = dp_all_reduce(rights)
    grad_up_right = rights[:group_up]
    grad_down_right = rights[group_up:]
    return (layer_out, grad_tokens, grad_up_left, grad_up_right, grad_down_left, grad_down_right)


def solution(mesh):
    fine = split_mesh(mesh)
    row = P(DP_AXES, FEAT_AXES)
    weight = P(FEAT_AXES, DP_AXES, None)
    mixer = P(FEAT_AXES, None, None)
    return jax.shard_map(
        on_device,
        mesh=fine,
        in_specs=(row, weight, mixer, weight, mixer, row),
        out_specs=(row, row, weight, mixer, weight, mixer),
        check_vma=False,
    )
```

```python
import jax
import jax.numpy as jnp
import numpy as np
from jax import lax
from jax.sharding import Mesh
from jax.sharding import PartitionSpec as P

TILE_UP = 128
TILE_DOWN = 32

DP_AXES = ("z", "ylo", "core")
FEAT_AXES = ("yhi", "x")


def split_mesh(mesh):
    n_dp = mesh.shape["dp"]
    n_feat = mesh.shape["feat"]
    sizes = (n_dp // 4, 2, 2, n_feat // 4, 4)
    devices = np.asarray(mesh.devices).reshape(sizes)
    return Mesh(devices, DP_AXES + FEAT_AXES)


def exchange(wired):
    return lax.all_to_all(wired, FEAT_AXES, 1, 1, tiled=True)


def shift(value, axis, step):
    n = lax.axis_size(axis)
    return lax.ppermute(value, axis, [(i, (i + step) % n) for i in range(n)])


def swap(value, axis, mask):
    n = lax.axis_size(axis)
    return lax.ppermute(value, axis, [(i, i ^ mask) for i in range(n)])


def z_ring_reduce_scatter(x):
    n = x.shape[0]
    me = lax.axis_index("z")
    n_fwd = n // 2
    n_bwd = n - 1 - n_fwd
    fwd = None
    bwd = None
    for step in range(1, n_fwd + 1):
        own = lax.dynamic_index_in_dim(x, (me + n_fwd + 1 - step) % n, 0, keepdims=False)
        fwd = shift(own if fwd is None else fwd + own, "z", 1)
        if step <= n_bwd:
            own = lax.dynamic_index_in_dim(x, (me - n_bwd - 1 + step) % n, 0, keepdims=False)
            bwd = shift(own if bwd is None else bwd + own, "z", -1)
    return fwd + bwd + lax.dynamic_index_in_dim(x, me, 0, keepdims=False)


def z_ring_all_gather(chunk):
    n = lax.axis_size("z")
    me = lax.axis_index("z")
    out = jnp.zeros((n,) + chunk.shape, chunk.dtype)
    out = lax.dynamic_update_index_in_dim(out, chunk, me, 0)
    fwd = chunk
    bwd = chunk
    half = n // 2
    for step in range(1, half):
        fwd = shift(fwd, "z", 1)
        bwd = shift(bwd, "z", -1)
        out = lax.dynamic_update_index_in_dim(out, fwd, (me - step) % n, 0)
        out = lax.dynamic_update_index_in_dim(out, bwd, (me + step) % n, 0)
    lo, _ = jnp.split(fwd, 2, axis=-1)
    _, hi = jnp.split(bwd, 2, axis=-1)
    last = jnp.concatenate([shift(lo, "z", 1), shift(hi, "z", -1)], axis=-1)
    out = lax.dynamic_update_index_in_dim(out, last, (me + half) % n, 0)
    return out


def dp_reduce_scatter(part):
    rows = part.shape[0]
    rest = part.shape[1:]
    n_z = lax.axis_size("z")
    x = part.reshape((n_z, 2, 2, rows // (4 * n_z)) + rest)
    core = lax.axis_index("core")
    mine = lax.dynamic_index_in_dim(x, core, 2, keepdims=False)
    other = lax.dynamic_index_in_dim(x, 1 - core, 2, keepdims=False)
    x = mine + swap(other, "core", 1)
    x = z_ring_reduce_scatter(x)
    ylo = lax.axis_index("ylo")
    mine = lax.dynamic_index_in_dim(x, ylo, 0, keepdims=False)
    other = lax.dynamic_index_in_dim(x, 1 - ylo, 0, keepdims=False)
    return mine + swap(other, "ylo", 1)


def dp_all_gather(local):
    ylo = lax.axis_index("ylo")
    got = swap(local, "ylo", 1)
    pair = jnp.where(ylo == 0, jnp.stack([local, got]), jnp.stack([got, local]))
    ring = z_ring_all_gather(pair)
    core = lax.axis_index("core")
    other = swap(ring, "core", 1)
    both = jnp.where(core == 0, jnp.stack([ring, other], 2), jnp.stack([other, ring], 2))
    return both.reshape((-1,) + local.shape[1:])


def dp_all_reduce(x):
    mask = lax.axis_size("z") // 2
    while mask >= 1:
        x = x + swap(x, "z", mask)
        mask //= 2
    x = x + swap(x, "ylo", 1)
    return x + swap(x, "core", 1)


def to_wire(blocks, feat_count):
    tok_rows, local_blocks, full_width = blocks.shape
    piece = full_width // feat_count
    shaped = blocks.reshape(tok_rows, local_blocks, feat_count, piece).transpose(0, 2, 1, 3)
    return shaped.reshape(tok_rows, feat_count, local_blocks * piece)


def from_wire(wired, local_blocks):
    tok_rows, feat_count, line_len = wired.shape
    piece = line_len // local_blocks
    shaped = wired.reshape(tok_rows, feat_count, local_blocks, piece).transpose(0, 2, 1, 3)
    return shaped.reshape(tok_rows, local_blocks, feat_count * piece)


def on_device(tokens, up_left, up_right, down_left, down_right, layer_grad):
    tok_rows = tokens.shape[0]
    local_blocks = up_left.shape[0]
    hidden_width = up_left.shape[2]
    block_width = down_left.shape[2]
    blocks_all = up_right.shape[1]
    group_up = up_right.shape[0]
    group_down = down_right.shape[0]
    feat_count = lax.axis_size("yhi") * lax.axis_size("x")
    n_dp = lax.axis_size("z") * lax.axis_size("ylo") * lax.axis_size("core")
    grad_scale = float(tok_rows * n_dp) ** (-0.5)
    tiles_up = group_up // TILE_UP
    tiles_down = group_down // TILE_DOWN
    hidden_rows = down_left.shape[1]
    up_rows = up_left.shape[1]
    weights = jnp.concatenate(
        [up_left[0], down_left[0].reshape(up_rows, hidden_rows * block_width // up_rows)], axis=1
    )
    weights = dp_all_gather(weights)
    up_full = weights[:, :hidden_width][None]
    down_full = weights[:, hidden_width:].reshape(1, -1, block_width)
    token_blocks = tokens.reshape(tok_rows, local_blocks, block_width)
    identity = jnp.eye(group_down, dtype=jnp.bfloat16).reshape(group_down, tiles_down, TILE_DOWN)
    mix_matrix = jnp.einsum(
        "cjk,cal->jcakl", down_right, identity, preferred_element_type=jnp.float32
    )
    mix_matrix = mix_matrix.astype(jnp.bfloat16).reshape(
        blocks_all * group_down, blocks_all * group_down
    )
    grad_down_mixed = lax.dot_general(
        layer_grad, mix_matrix, (((1,), (1,)), ((), ())), preferred_element_type=jnp.float32
    ).astype(jnp.bfloat16)
    up_inner = jnp.einsum(
        "tbi,big->tbg", token_blocks, up_full, preferred_element_type=jnp.float32
    ).astype(jnp.bfloat16)
    up_piece = hidden_width // feat_count
    first = exchange(
        jnp.concatenate(
            [
                to_wire(up_inner, feat_count),
                grad_down_mixed.reshape(tok_rows, feat_count, local_blocks * group_down),
            ],
            axis=2,
        )
    )
    up_mixed = first[:, :, :up_piece]
    grad_down_inner = from_wire(first[:, :, up_piece:], local_blocks)
    preact = jnp.einsum("tjg,gjk->tkg", up_mixed, up_right, preferred_element_type=jnp.float32)
    sigmoid_val = jax.nn.sigmoid(preact)
    activated = (
        (preact * sigmoid_val)
        .reshape(tok_rows, blocks_all, tiles_up, TILE_UP)
        .transpose(0, 2, 1, 3)
    )
    hidden = activated.reshape(tok_rows, local_blocks, hidden_width).astype(jnp.bfloat16)
    down_inner = jnp.einsum(
        "tbh,bhc->tbc", hidden, down_full, preferred_element_type=jnp.float32
    ).astype(jnp.bfloat16)
    grad_hidden = jnp.einsum(
        "tbc,bhc->tbh", grad_down_inner, down_full, preferred_element_type=jnp.float32
    )
    grad_hidden = grad_hidden.reshape(tok_rows, tiles_up, blocks_all, TILE_UP).transpose(0, 2, 1, 3)
    grad_hidden = grad_hidden.reshape(tok_rows, blocks_all, group_up)
    grad_preact = (grad_hidden * sigmoid_val * (1.0 + preact * (1.0 - sigmoid_val))).astype(
        jnp.bfloat16
    )
    grad_up_mixed = jnp.einsum(
        "tkg,gjk->tjg", grad_preact, up_right, preferred_element_type=jnp.float32
    ).astype(jnp.bfloat16)
    right_up_term = (
        jnp.einsum("tjg,tkg->gjk", up_mixed, grad_preact, preferred_element_type=jnp.float32)
        * grad_scale
    )
    down_part = jnp.einsum(
        "tbh,tbc->hbc", hidden, grad_down_inner, preferred_element_type=jnp.float32
    )
    down_piece = block_width // feat_count
    second = exchange(
        jnp.concatenate([to_wire(down_inner, feat_count), grad_up_mixed], axis=2)
    )
    down_mixed = second[:, :, :down_piece].reshape(tok_rows, blocks_all * group_down)
    grad_up_inner = from_wire(second[:, :, down_piece:], local_blocks)
    layer_out = jnp.dot(down_mixed, mix_matrix, preferred_element_type=jnp.float32).astype(
        jnp.bfloat16
    )
    grad_by_group = layer_grad.reshape(tok_rows, tiles_down, blocks_all, TILE_DOWN).transpose(
        0, 2, 1, 3
    )
    grad_by_group = grad_by_group.reshape(tok_rows, blocks_all, group_down)
    right_down_term = (
        jnp.einsum(
            "tjc,tkc->cjk",
            down_mixed.reshape(tok_rows, blocks_all, group_down),
            grad_by_group,
            preferred_element_type=jnp.float32,
        )
        * grad_scale
    )
    grad_tokens = jnp.einsum(
        "tbg,big->tbi", grad_up_inner, up_full, preferred_element_type=jnp.float32
    ).astype(jnp.bfloat16)
    grad_tokens = grad_tokens.reshape(tok_rows, local_blocks * block_width)
    up_part = jnp.einsum(
        "tbi,tbg->ibg", token_blocks, grad_up_inner, preferred_element_type=jnp.float32
    )
    n_rows = up_part.shape[0] // up_rows
    parts = jnp.stack(
        [
            up_part.reshape(n_rows, up_rows, hidden_width),
            down_part.reshape(n_rows, up_rows, hidden_width),
        ],
        axis=1,
    )
    summed = dp_reduce_scatter(parts * grad_scale)[0]
    grad_up_left = summed[0][None]
    grad_down_left = summed[1].reshape(1, hidden_rows, block_width)
    rights = jnp.concatenate([right_up_term, right_down_term], axis=0)
    rights = dp_all_reduce(rights)
    grad_up_right = rights[:group_up]
    grad_down_right = rights[group_up:]
    return (layer_out, grad_tokens, grad_up_left, grad_up_right, grad_down_left, grad_down_right)


def solution(mesh):
    fine = split_mesh(mesh)
    row = P(DP_AXES, FEAT_AXES)
    weight = P(FEAT_AXES, DP_AXES, None)
    mixer = P(FEAT_AXES, None, None)
    return jax.shard_map(
        on_device,
        mesh=fine,
        in_specs=(row, weight, mixer, weight, mixer, row),
        out_specs=(row, row, weight, mixer, weight, mixer),
        check_vma=False,
    )
```

```python
import jax
import jax.numpy as jnp
import numpy as np
from jax import lax
from jax.sharding import Mesh
from jax.sharding import PartitionSpec as P

TILE_UP = 128
TILE_DOWN = 32

DP_AXES = ("z", "ylo", "core")
FEAT_AXES = ("yhi", "x")


def split_mesh(mesh):
    n_dp = mesh.shape["dp"]
    n_feat = mesh.shape["feat"]
    sizes = (n_dp // 4, 2, 2, n_feat // 4, 4)
    devices = np.asarray(mesh.devices).reshape(sizes)
    return Mesh(devices, DP_AXES + FEAT_AXES)


def exchange(wired):
    return lax.all_to_all(wired, FEAT_AXES, 1, 1, tiled=True)


def shift(value, axis, step):
    n = lax.axis_size(axis)
    return lax.ppermute(value, axis, [(i, (i + step) % n) for i in range(n)])


def swap(value, axis, mask):
    n = lax.axis_size(axis)
    return lax.ppermute(value, axis, [(i, i ^ mask) for i in range(n)])


def z_ring_reduce_scatter(x):
    n = x.shape[0]
    me = lax.axis_index("z")
    n_fwd = n // 2
    n_bwd = n - 1 - n_fwd
    fwd = None
    bwd = None
    for step in range(1, n_fwd + 1):
        own = lax.dynamic_index_in_dim(x, (me + n_fwd + 1 - step) % n, 0, keepdims=False)
        fwd = own if fwd is None else fwd + own
        if step <= n_bwd:
            own = lax.dynamic_index_in_dim(x, (me - n_bwd - 1 + step) % n, 0, keepdims=False)
            bwd = own if bwd is None else bwd + own
            fwd, bwd = lax.optimization_barrier((fwd, bwd))
            bwd = shift(bwd, "z", -1)
        fwd = shift(fwd, "z", 1)
    return fwd + bwd + lax.dynamic_index_in_dim(x, me, 0, keepdims=False)


def z_ring_all_gather(chunk):
    n = lax.axis_size("z")
    me = lax.axis_index("z")
    out = jnp.zeros((n,) + chunk.shape, chunk.dtype)
    out = lax.dynamic_update_index_in_dim(out, chunk, me, 0)
    fwd = chunk
    bwd = chunk
    half = n // 2
    for step in range(1, half):
        fwd = shift(fwd, "z", 1)
        bwd = shift(bwd, "z", -1)
        out = lax.dynamic_update_index_in_dim(out, fwd, (me - step) % n, 0)
        out = lax.dynamic_update_index_in_dim(out, bwd, (me + step) % n, 0)
    lo, _ = jnp.split(fwd, 2, axis=-1)
    _, hi = jnp.split(bwd, 2, axis=-1)
    last = jnp.concatenate([shift(lo, "z", 1), shift(hi, "z", -1)], axis=-1)
    out = lax.dynamic_update_index_in_dim(out, last, (me + half) % n, 0)
    return out


def dp_reduce_scatter(part):
    rows = part.shape[0]
    rest = part.shape[1:]
    n_z = lax.axis_size("z")
    x = part.reshape((n_z, 2, 2, rows // (4 * n_z)) + rest)
    core = lax.axis_index("core")
    mine = lax.dynamic_index_in_dim(x, core, 2, keepdims=False)
    other = lax.dynamic_index_in_dim(x, 1 - core, 2, keepdims=False)
    x = mine + swap(other, "core", 1)
    x = z_ring_reduce_scatter(x)
    ylo = lax.axis_index("ylo")
    mine = lax.dynamic_index_in_dim(x, ylo, 0, keepdims=False)
    other = lax.dynamic_index_in_dim(x, 1 - ylo, 0, keepdims=False)
    return mine + swap(other, "ylo", 1)


def dp_all_gather(local):
    ylo = lax.axis_index("ylo")
    got = swap(local, "ylo", 1)
    pair = jnp.where(ylo == 0, jnp.stack([local, got]), jnp.stack([got, local]))
    ring = z_ring_all_gather(pair)
    core = lax.axis_index("core")
    other = swap(ring, "core", 1)
    both = jnp.where(core == 0, jnp.stack([ring, other], 2), jnp.stack([other, ring], 2))
    return both.reshape((-1,) + local.shape[1:])


def dp_all_reduce(x):
    mask = lax.axis_size("z") // 2
    while mask >= 1:
        x = x + swap(x, "z", mask)
        mask //= 2
    x = x + swap(x, "ylo", 1)
    return x + swap(x, "core", 1)


def to_wire(blocks, feat_count):
    tok_rows, local_blocks, full_width = blocks.shape
    piece = full_width // feat_count
    shaped = blocks.reshape(tok_rows, local_blocks, feat_count, piece).transpose(0, 2, 1, 3)
    return shaped.reshape(tok_rows, feat_count, local_blocks * piece)


def from_wire(wired, local_blocks):
    tok_rows, feat_count, line_len = wired.shape
    piece = line_len // local_blocks
    shaped = wired.reshape(tok_rows, feat_count, local_blocks, piece).transpose(0, 2, 1, 3)
    return shaped.reshape(tok_rows, local_blocks, feat_count * piece)


def on_device(tokens, up_left, up_right, down_left, down_right, layer_grad):
    tok_rows = tokens.shape[0]
    local_blocks = up_left.shape[0]
    hidden_width = up_left.shape[2]
    block_width = down_left.shape[2]
    blocks_all = up_right.shape[1]
    group_up = up_right.shape[0]
    group_down = down_right.shape[0]
    feat_count = lax.axis_size("yhi") * lax.axis_size("x")
    n_dp = lax.axis_size("z") * lax.axis_size("ylo") * lax.axis_size("core")
    grad_scale = float(tok_rows * n_dp) ** (-0.5)
    tiles_up = group_up // TILE_UP
    tiles_down = group_down // TILE_DOWN
    hidden_rows = down_left.shape[1]
    up_rows = up_left.shape[1]
    weights = jnp.concatenate(
        [up_left[0], down_left[0].reshape(up_rows, hidden_rows * block_width // up_rows)], axis=1
    )
    weights = dp_all_gather(weights)
    up_full = weights[:, :hidden_width][None]
    down_full = weights[:, hidden_width:].reshape(1, -1, block_width)
    token_blocks = tokens.reshape(tok_rows, local_blocks, block_width)
    identity = jnp.eye(group_down, dtype=jnp.bfloat16).reshape(group_down, tiles_down, TILE_DOWN)
    mix_matrix = jnp.einsum(
        "cjk,cal->jcakl", down_right, identity, preferred_element_type=jnp.float32
    )
    mix_matrix = mix_matrix.astype(jnp.bfloat16).reshape(
        blocks_all * group_down, blocks_all * group_down
    )
    grad_down_mixed = lax.dot_general(
        layer_grad, mix_matrix, (((1,), (1,)), ((), ())), preferred_element_type=jnp.float32
    ).astype(jnp.bfloat16)
    up_inner = jnp.einsum(
        "tbi,big->tbg", token_blocks, up_full, preferred_element_type=jnp.float32
    ).astype(jnp.bfloat16)
    up_piece = hidden_width // feat_count
    first = exchange(
        jnp.concatenate(
            [
                to_wire(up_inner, feat_count),
                grad_down_mixed.reshape(tok_rows, feat_count, local_blocks * group_down),
            ],
            axis=2,
        )
    )
    up_mixed = first[:, :, :up_piece]
    grad_down_inner = from_wire(first[:, :, up_piece:], local_blocks)
    preact = jnp.einsum("tjg,gjk->tkg", up_mixed, up_right, preferred_element_type=jnp.float32)
    sigmoid_val = jax.nn.sigmoid(preact)
    activated = (
        (preact * sigmoid_val)
        .reshape(tok_rows, blocks_all, tiles_up, TILE_UP)
        .transpose(0, 2, 1, 3)
    )
    hidden = activated.reshape(tok_rows, local_blocks, hidden_width).astype(jnp.bfloat16)
    down_inner = jnp.einsum(
        "tbh,bhc->tbc", hidden, down_full, preferred_element_type=jnp.float32
    ).astype(jnp.bfloat16)
    grad_hidden = jnp.einsum(
        "tbc,bhc->tbh", grad_down_inner, down_full, preferred_element_type=jnp.float32
    )
    grad_hidden = grad_hidden.reshape(tok_rows, tiles_up, blocks_all, TILE_UP).transpose(0, 2, 1, 3)
    grad_hidden = grad_hidden.reshape(tok_rows, blocks_all, group_up)
    grad_preact = (grad_hidden * sigmoid_val * (1.0 + preact * (1.0 - sigmoid_val))).astype(
        jnp.bfloat16
    )
    grad_up_mixed = jnp.einsum(
        "tkg,gjk->tjg", grad_preact, up_right, preferred_element_type=jnp.float32
    ).astype(jnp.bfloat16)
    right_up_term = (
        jnp.einsum("tjg,tkg->gjk", up_mixed, grad_preact, preferred_element_type=jnp.float32)
        * grad_scale
    )
    down_part = jnp.einsum(
        "tbh,tbc->hbc", hidden, grad_down_inner, preferred_element_type=jnp.float32
    )
    down_piece = block_width // feat_count
    second = exchange(
        jnp.concatenate([to_wire(down_inner, feat_count), grad_up_mixed], axis=2)
    )
    down_mixed = second[:, :, :down_piece].reshape(tok_rows, blocks_all * group_down)
    grad_up_inner = from_wire(second[:, :, down_piece:], local_blocks)
    layer_out = jnp.dot(down_mixed, mix_matrix, preferred_element_type=jnp.float32).astype(
        jnp.bfloat16
    )
    grad_by_group = layer_grad.reshape(tok_rows, tiles_down, blocks_all, TILE_DOWN).transpose(
        0, 2, 1, 3
    )
    grad_by_group = grad_by_group.reshape(tok_rows, blocks_all, group_down)
    right_down_term = (
        jnp.einsum(
            "tjc,tkc->cjk",
            down_mixed.reshape(tok_rows, blocks_all, group_down),
            grad_by_group,
            preferred_element_type=jnp.float32,
        )
        * grad_scale
    )
    grad_tokens = jnp.einsum(
        "tbg,big->tbi", grad_up_inner, up_full, preferred_element_type=jnp.float32
    ).astype(jnp.bfloat16)
    grad_tokens = grad_tokens.reshape(tok_rows, local_blocks * block_width)
    up_part = jnp.einsum(
        "tbi,tbg->ibg", token_blocks, grad_up_inner, preferred_element_type=jnp.float32
    )
    n_rows = up_part.shape[0] // up_rows
    parts = jnp.stack(
        [
            up_part.reshape(n_rows, up_rows, hidden_width),
            down_part.reshape(n_rows, up_rows, hidden_width),
        ],
        axis=1,
    )
    summed = dp_reduce_scatter(parts * grad_scale)[0]
    grad_up_left = summed[0][None]
    grad_down_left = summed[1].reshape(1, hidden_rows, block_width)
    rights = jnp.concatenate([right_up_term, right_down_term], axis=0)
    rights = dp_all_reduce(rights)
    grad_up_right = rights[:group_up]
    grad_down_right = rights[group_up:]
    return (layer_out, grad_tokens, grad_up_left, grad_up_right, grad_down_left, grad_down_right)


def solution(mesh):
    fine = split_mesh(mesh)
    row = P(DP_AXES, FEAT_AXES)
    weight = P(FEAT_AXES, DP_AXES, None)
    mixer = P(FEAT_AXES, None, None)
    return jax.shard_map(
        on_device,
        mesh=fine,
        in_specs=(row, weight, mixer, weight, mixer, row),
        out_specs=(row, row, weight, mixer, weight, mixer),
        check_vma=False,
    )
```

```python
import jax
import jax.numpy as jnp
import numpy as np
from jax import lax
from jax.sharding import Mesh
from jax.sharding import PartitionSpec as P

TILE_UP = 128
TILE_DOWN = 32

DP_AXES = ("z", "ylo", "core")
FEAT_AXES = ("yhi", "x")


def split_mesh(mesh):
    n_dp = mesh.shape["dp"]
    n_feat = mesh.shape["feat"]
    sizes = (n_dp // 4, 2, 2, n_feat // 4, 4)
    devices = np.asarray(mesh.devices).reshape(sizes)
    return Mesh(devices, DP_AXES + FEAT_AXES)


def exchange(wired):
    return lax.all_to_all(wired, FEAT_AXES, 1, 1, tiled=True)


def shift(value, axis, step):
    n = lax.axis_size(axis)
    return lax.ppermute(value, axis, [(i, (i + step) % n) for i in range(n)])


def swap(value, axis, mask):
    n = lax.axis_size(axis)
    return lax.ppermute(value, axis, [(i, i ^ mask) for i in range(n)])


def z_ring_reduce_scatter(x):
    n = x.shape[0]
    me = lax.axis_index("z")
    n_fwd = n // 2
    n_bwd = n - 1 - n_fwd
    fwd = None
    bwd = None
    for step in range(1, n_fwd + 1):
        own = lax.dynamic_index_in_dim(x, (me + n_fwd + 1 - step) % n, 0, keepdims=False)
        fwd = shift(own if fwd is None else fwd + own, "z", 1)
        if step <= n_bwd:
            own = lax.dynamic_index_in_dim(x, (me - n_bwd - 1 + step) % n, 0, keepdims=False)
            bwd = shift(own if bwd is None else bwd + own, "z", -1)
    return fwd + bwd + lax.dynamic_index_in_dim(x, me, 0, keepdims=False)


def z_ring_all_gather(chunk):
    n = lax.axis_size("z")
    me = lax.axis_index("z")
    out = jnp.zeros((n,) + chunk.shape, chunk.dtype)
    out = lax.dynamic_update_index_in_dim(out, chunk, me, 0)
    fwd = chunk
    bwd = chunk
    half = n // 2
    for step in range(1, half):
        fwd = shift(fwd, "z", 1)
        bwd = shift(bwd, "z", -1)
        out = lax.dynamic_update_index_in_dim(out, fwd, (me - step) % n, 0)
        out = lax.dynamic_update_index_in_dim(out, bwd, (me + step) % n, 0)
    last = shift(fwd, "z", 1)
    out = lax.dynamic_update_index_in_dim(out, last, (me + half) % n, 0)
    return out


def dp_reduce_scatter(part):
    rows = part.shape[0]
    rest = part.shape[1:]
    n_z = lax.axis_size("z")
    x = part.reshape((n_z, 2, 2, rows // (4 * n_z)) + rest)
    core = lax.axis_index("core")
    mine = lax.dynamic_index_in_dim(x, core, 2, keepdims=False)
    other = lax.dynamic_index_in_dim(x, 1 - core, 2, keepdims=False)
    x = mine + swap(other, "core", 1)
    x = z_ring_reduce_scatter(x)
    ylo = lax.axis_index("ylo")
    mine = lax.dynamic_index_in_dim(x, ylo, 0, keepdims=False)
    other = lax.dynamic_index_in_dim(x, 1 - ylo, 0, keepdims=False)
    return mine + swap(other, "ylo", 1)


def dp_all_gather(local):
    ylo = lax.axis_index("ylo")
    got = swap(local, "ylo", 1)
    pair = jnp.where(ylo == 0, jnp.stack([local, got]), jnp.stack([got, local]))
    ring = z_ring_all_gather(pair)
    core = lax.axis_index("core")
    other = swap(ring, "core", 1)
    both = jnp.where(core == 0, jnp.stack([ring, other], 2), jnp.stack([other, ring], 2))
    return both.reshape((-1,) + local.shape[1:])


def dp_all_reduce(x):
    mask = lax.axis_size("z") // 2
    while mask >= 1:
        x = x + swap(x, "z", mask)
        mask //= 2
    x = x + swap(x, "ylo", 1)
    return x + swap(x, "core", 1)


def to_wire(blocks, feat_count):
    tok_rows, local_blocks, full_width = blocks.shape
    piece = full_width // feat_count
    shaped = blocks.reshape(tok_rows, local_blocks, feat_count, piece).transpose(0, 2, 1, 3)
    return shaped.reshape(tok_rows, feat_count, local_blocks * piece)


def from_wire(wired, local_blocks):
    tok_rows, feat_count, line_len = wired.shape
    piece = line_len // local_blocks
    shaped = wired.reshape(tok_rows, feat_count, local_blocks, piece).transpose(0, 2, 1, 3)
    return shaped.reshape(tok_rows, local_blocks, feat_count * piece)


def on_device(tokens, up_left, up_right, down_left, down_right, layer_grad):
    tok_rows = tokens.shape[0]
    local_blocks = up_left.shape[0]
    hidden_width = up_left.shape[2]
    block_width = down_left.shape[2]
    blocks_all = up_right.shape[1]
    group_up = up_right.shape[0]
    group_down = down_right.shape[0]
    feat_count = lax.axis_size("yhi") * lax.axis_size("x")
    n_dp = lax.axis_size("z") * lax.axis_size("ylo") * lax.axis_size("core")
    grad_scale = float(tok_rows * n_dp) ** (-0.5)
    tiles_up = group_up // TILE_UP
    tiles_down = group_down // TILE_DOWN
    hidden_rows = down_left.shape[1]
    up_rows = up_left.shape[1]
    weights = jnp.concatenate(
        [up_left[0], down_left[0].reshape(up_rows, hidden_rows * block_width // up_rows)], axis=1
    )
    weights = dp_all_gather(weights)
    up_full = weights[:, :hidden_width][None]
    down_full = weights[:, hidden_width:].reshape(1, -1, block_width)
    token_blocks = tokens.reshape(tok_rows, local_blocks, block_width)
    identity = jnp.eye(group_down, dtype=jnp.bfloat16).reshape(group_down, tiles_down, TILE_DOWN)
    mix_matrix = jnp.einsum(
        "cjk,cal->jcakl", down_right, identity, preferred_element_type=jnp.float32
    )
    mix_matrix = mix_matrix.astype(jnp.bfloat16).reshape(
        blocks_all * group_down, blocks_all * group_down
    )
    grad_down_mixed = lax.dot_general(
        layer_grad, mix_matrix, (((1,), (1,)), ((), ())), preferred_element_type=jnp.float32
    ).astype(jnp.bfloat16)
    up_inner = jnp.einsum(
        "tbi,big->tbg", token_blocks, up_full, preferred_element_type=jnp.float32
    ).astype(jnp.bfloat16)
    up_piece = hidden_width // feat_count
    first = exchange(
        jnp.concatenate(
            [
                to_wire(up_inner, feat_count),
                grad_down_mixed.reshape(tok_rows, feat_count, local_blocks * group_down),
            ],
            axis=2,
        )
    )
    up_mixed = first[:, :, :up_piece]
    grad_down_inner = from_wire(first[:, :, up_piece:], local_blocks)
    preact = jnp.einsum("tjg,gjk->tkg", up_mixed, up_right, preferred_element_type=jnp.float32)
    sigmoid_val = jax.nn.sigmoid(preact)
    activated = (
        (preact * sigmoid_val)
        .reshape(tok_rows, blocks_all, tiles_up, TILE_UP)
        .transpose(0, 2, 1, 3)
    )
    hidden = activated.reshape(tok_rows, local_blocks, hidden_width).astype(jnp.bfloat16)
    down_inner = jnp.einsum(
        "tbh,bhc->tbc", hidden, down_full, preferred_element_type=jnp.float32
    ).astype(jnp.bfloat16)
    grad_hidden = jnp.einsum(
        "tbc,bhc->tbh", grad_down_inner, down_full, preferred_element_type=jnp.float32
    )
    grad_hidden = grad_hidden.reshape(tok_rows, tiles_up, blocks_all, TILE_UP).transpose(0, 2, 1, 3)
    grad_hidden = grad_hidden.reshape(tok_rows, blocks_all, group_up)
    grad_preact = (grad_hidden * sigmoid_val * (1.0 + preact * (1.0 - sigmoid_val))).astype(
        jnp.bfloat16
    )
    grad_up_mixed = jnp.einsum(
        "tkg,gjk->tjg", grad_preact, up_right, preferred_element_type=jnp.float32
    ).astype(jnp.bfloat16)
    right_up_term = (
        jnp.einsum("tjg,tkg->gjk", up_mixed, grad_preact, preferred_element_type=jnp.float32)
        * grad_scale
    )
    down_part = jnp.einsum(
        "tbh,tbc->hbc", hidden, grad_down_inner, preferred_element_type=jnp.float32
    )
    down_piece = block_width // feat_count
    second = exchange(
        jnp.concatenate([to_wire(down_inner, feat_count), grad_up_mixed], axis=2)
    )
    down_mixed = second[:, :, :down_piece].reshape(tok_rows, blocks_all * group_down)
    grad_up_inner = from_wire(second[:, :, down_piece:], local_blocks)
    layer_out = jnp.dot(down_mixed, mix_matrix, preferred_element_type=jnp.float32).astype(
        jnp.bfloat16
    )
    grad_by_group = layer_grad.reshape(tok_rows, tiles_down, blocks_all, TILE_DOWN).transpose(
        0, 2, 1, 3
    )
    grad_by_group = grad_by_group.reshape(tok_rows, blocks_all, group_down)
    right_down_term = (
        jnp.einsum(
            "tjc,tkc->cjk",
            down_mixed.reshape(tok_rows, blocks_all, group_down),
            grad_by_group,
            preferred_element_type=jnp.float32,
        )
        * grad_scale
    )
    grad_tokens = jnp.einsum(
        "tbg,big->tbi", grad_up_inner, up_full, preferred_element_type=jnp.float32
    ).astype(jnp.bfloat16)
    grad_tokens = grad_tokens.reshape(tok_rows, local_blocks * block_width)
    up_part = jnp.einsum(
        "tbi,tbg->ibg", token_blocks, grad_up_inner, preferred_element_type=jnp.float32
    )
    n_rows = up_part.shape[0] // up_rows
    parts = jnp.stack(
        [
            up_part.reshape(n_rows, up_rows, hidden_width),
            down_part.reshape(n_rows, up_rows, hidden_width),
        ],
        axis=1,
    )
    summed = dp_reduce_scatter(parts * grad_scale)[0]
    grad_up_left = summed[0][None]
    grad_down_left = summed[1].reshape(1, hidden_rows, block_width)
    rights = jnp.concatenate([right_up_term, right_down_term], axis=0)
    rights = dp_all_reduce(rights)
    grad_up_right = rights[:group_up]
    grad_down_right = rights[group_up:]
    return (layer_out, grad_tokens, grad_up_left, grad_up_right, grad_down_left, grad_down_right)


def solution(mesh):
    fine = split_mesh(mesh)
    row = P(DP_AXES, FEAT_AXES)
    weight = P(FEAT_AXES, DP_AXES, None)
    mixer = P(FEAT_AXES, None, None)
    return jax.shard_map(
        on_device,
        mesh=fine,
        in_specs=(row, weight, mixer, weight, mixer, row),
        out_specs=(row, row, weight, mixer, weight, mixer),
        check_vma=False,
    )
```
